256 devices in a mesh: gx: 8 (over y_hi, x), gy: 32 (over z, y_lo, core).
Axes of the slice: x: 4, y: 4 (y_hi: 2, y_lo: 2; y = y_hi * 2 + y_lo), z: 8, core: 2. Of those that a mesh axis runs over, the one named last changes fastest.
Arguments:
- f_start: float32 [19, 4, 1024, 1024], P(None, None, 'gy', 'gx'), may hold values from 0.022 to 0.4, as said below
- cotangent: bfloat16 [19, 4, 1024, 1024], P(None, None, 'gy', 'gx'), may hold values from -6 to 6
- porosity: float32 [8, 32, 16], P('gx', 'gy'), may hold values from 0.1 to 0.9
- brick_ids: int32 [8, 32, 64], P('gx', 'gy'), may hold values from 0 to 127, as said below
- brick_slot: int32 [8, 32, 64], P('gx', 'gy'), may hold values from 0 to 15
Outputs:
- start_grad: float32 [19, 4, 1024, 1024], P(None, None, 'gy', 'gx')
- porosity_grad: float32 [8, 32, 16], P('gx', 'gy')
The draws below stay inside these ranges and needn't reach their ends.
Inputs may be any that keep to these rules, and one draw needn't show every extreme that they name: `f_start`: each population is w_q times a factor between 0.8 and 1.2, w_q the weight of its direction. `brick_ids`: each device lists 64 distinct bricks of its own block; brick b covers layer b // 32, row b % 32 and all 128 cells along x of that block; device (0, 0) lists the last brick and device (0, 1) the first.
All inputs are finite; a program needn't handle non-finite values.
Results may differ from the reference program's by a relative error of at most 0.0003.
Values sent between devices are 32-bit elements; how exact they have to be, the bound alone decides.
No kernel may reach another device: no remote copies, remote signals or barrier semaphores. Data moves between devices by JAX's collectives and lax.ppermute only.
A program may use at most 64 MiB of HBM per device.

```python
import jax
import jax.numpy as jnp
import numpy as np
from jax import lax

Z = 4
CX = 128
CY = 32
NB = 64
SLOTS = 16
NX = 1024
NY = 1024
N_GX = 8
N_GY = 32


WEIGHT_TABLE = np.array([1.0 / 3.0] + [1.0 / 18.0] * 6 + [1.0 / 36.0] * 12, dtype=np.float32)


def draw_f_start(key, part):
    shape = (19, Z, NY, NX)
    weights = jnp.asarray(WEIGHT_TABLE)[:, None, None, None]
    factor = jax.random.uniform(key, shape, jnp.float32, 0.8, 1.2)
    return weights * factor


def draw_brick_ids(key, part):
    brick_count = Z * CY * (CX // 128)
    device_count = N_GX * N_GY
    key_list = jax.random.split(key, device_count)
    orders = jax.vmap(lambda single: jax.random.permutation(single, brick_count))(key_list)
    device_row = jnp.arange(device_count, dtype=jnp.int32)[:, None]
    leading = orders[:, :1]
    to_last = (orders + (brick_count - 1 - leading)) % brick_count
    to_first = (orders - leading) % brick_count
    orders = jnp.where(device_row == 0, to_last, jnp.where(device_row == 1, to_first, orders))
    return orders[:, :NB].reshape(N_GX, N_GY, NB).astype(jnp.int32)


def place_ends(values, stream_key, low, high):
    longest = values.shape.index(max(values.shape))
    spots = []
    for shift in (0, 1):
        where = [jax.random.randint(jax.random.fold_in(stream_key, axis), (), 0, length) for axis, length in enumerate(values.shape)]
        where[longest] = (where[longest] + shift) % values.shape[longest]
        spots.append(tuple(where))
    return values.at[spots[0]].set(low).at[spots[1]].set(high)


def block_levels(stream_key, extent, cuts, smallest, largest):
    factor_of, own = 1.0, jax.random.fold_in(stream_key, 6)
    for axis_at, parts in cuts:
        draws = jnp.exp(jax.random.uniform(jax.random.fold_in(own, axis_at), (parts,), jnp.float32, smallest / len(cuts), largest / len(cuts)))
        factor_of = factor_of * jnp.repeat(draws, extent[axis_at] // parts).reshape([-1 if axis == axis_at else 1 for axis in range(len(extent))])
    return factor_of


def noise(rng, shape, scale, limit, cuts=(), held_as=jnp.bfloat16):
    gain = block_levels(rng, shape, cuts, -0.22, 0.18) if cuts else 1.0
    drawn = jax.random.normal(rng, shape, jnp.float32) * scale * gain
    return jnp.minimum(jnp.maximum(drawn, -limit), limit).astype(held_as)


def setup_inputs(seed: int = 0) -> dict:
    arg_keys = jax.random.split(jax.random.key(seed), 6)
    f_start = draw_f_start(jax.random.fold_in(arg_keys[5], 71), 0)
    cotangent = noise(arg_keys[1], (19, Z, NY, NX), 1.0, 6.0, ((2, 32), (3, 8)))
    porosity = jnp.clip(0.1 + 0.79999997 * jax.random.uniform(arg_keys[2], (N_GX, N_GY, SLOTS), jnp.float32) ** block_levels(arg_keys[2], (N_GX, N_GY, SLOTS), ((0, 8), (1, 32)), -0.2, 0.2), 0.1, 0.9)
    brick_ids = draw_brick_ids(jax.random.fold_in(arg_keys[5], 71), 0)
    brick_slot = place_ends(jax.random.randint(arg_keys[4], (N_GX, N_GY, NB), 0, SLOTS), jax.random.fold_in(arg_keys[4], 1), 0, SLOTS - 1).astype(jnp.int32)
    return {"f_start": f_start, "cotangent": cotangent, "porosity": porosity, "brick_ids": brick_ids, "brick_slot": brick_slot}


DIR_X = np.array([0, 1, -1, 0, 0, 0, 0, 1, -1, 1, -1, 1, -1, 1, -1, 0, 0, 0, 0])
DIR_Y = np.array([0, 0, 0, 1, -1, 0, 0, 1, 1, -1, -1, 0, 0, 0, 0, 1, -1, 1, -1])
DIR_Z = np.array([0, 0, 0, 0, 0, 1, -1, 0, 0, 0, 0, 1, 1, -1, -1, 1, 1, -1, -1])
WEIGHTS = np.array([1.0 / 3.0] + [1.0 / 18.0] * 6 + [1.0 / 36.0] * 12)
RELAX_RATE = 0.8

def column(values):
    return np.asarray(values, np.float32)[:, None, None, None]

def collide(field, solid):
    density = lax.optimization_barrier(jnp.sum(field, axis=0))
    inverse = (1.0 - solid) / density
    vel_x = lax.optimization_barrier(jnp.sum(field * column(DIR_X), axis=0)) * inverse
    vel_y = lax.optimization_barrier(jnp.sum(field * column(DIR_Y), axis=0)) * inverse
    vel_z = lax.optimization_barrier(jnp.sum(field * column(DIR_Z), axis=0)) * inverse
    along = column(DIR_X) * vel_x + column(DIR_Y) * vel_y + column(DIR_Z) * vel_z
    square = vel_x * vel_x + vel_y * vel_y + vel_z * vel_z
    balance = column(WEIGHTS) * density * (1.0 + 3.0 * along + 4.5 * along * along - 1.5 * square)
    return field - RELAX_RATE * (field - balance)

def collide_layers(field, solid):
    moved = jnp.moveaxis(field, 1, 0)
    result = lax.map(lambda pair: collide(pair[0][:, None], pair[1][None])[:, 0], (moved, solid))
    return jnp.moveaxis(result, 0, 1)

def collide_back(field, solid, incoming):

    def one_layer(items):
        layer, solid_layer, cot_layer = items
        ignored, undo_layer = jax.vjp(collide, layer[:, None], solid_layer[None])
        grad_field, grad_solid = undo_layer(cot_layer[:, None])
        return (grad_field[:, 0], grad_solid[0])
    grad_field, grad_solid = lax.map(one_layer, (jnp.moveaxis(field, 1, 0), solid, jnp.moveaxis(incoming, 1, 0)))
    return (jnp.moveaxis(grad_field, 0, 1), grad_solid)

def stream(field, sign):
    moved = []
    for lane in range(19):
        offset = (sign * int(DIR_Z[lane]), sign * int(DIR_Y[lane]), sign * int(DIR_X[lane]))
        moved.append(jnp.roll(field[lane], offset, axis=(0, 1, 2)))
    return jnp.stack(moved)

def reference(f_start, cotangent, porosity, brick_ids, brick_slot):
    tile_count = CX // 128
    brick_count = Z * CY * tile_count
    brick_hit = (brick_ids[..., None] == jnp.arange(brick_count, dtype=jnp.int32)).astype(jnp.float32)
    slot_hit = (brick_slot[..., None] == jnp.arange(SLOTS, dtype=jnp.int32)).astype(jnp.float32)
    brick_value = lax.optimization_barrier(jnp.sum(slot_hit * porosity[:, :, None, :], axis=3))
    tile_value = lax.optimization_barrier(jnp.sum(brick_hit * brick_value[..., None], axis=2))
    grid_tiles = tile_value.reshape(N_GX, N_GY, Z, CY, tile_count).transpose(2, 1, 3, 0, 4).reshape(Z, NY, NX // 128)
    solid = jnp.broadcast_to(grid_tiles[..., None], (Z, NY, NX // 128, 128)).reshape(Z, NY, NX)
    after_one = stream(collide_layers(f_start, solid), 1)
    back_two = stream(cotangent.astype(jnp.float32), -1)
    back_one, solid_bar_two = collide_back(after_one, solid, back_two)
    start_grad, solid_bar_one = collide_back(f_start, solid, stream(back_one, -1))
    solid_bar = solid_bar_one + solid_bar_two
    tile_sums = solid_bar.reshape(Z, N_GY, CY, N_GX, tile_count, 128).sum(axis=5)
    tile_sums = tile_sums.transpose(3, 1, 0, 2, 4).reshape(N_GX, N_GY, brick_count)
    brick_sum = lax.optimization_barrier(jnp.sum(brick_hit * tile_sums[:, :, None, :], axis=3))
    porosity_grad = lax.optimization_barrier(jnp.sum(slot_hit * brick_sum[..., None], axis=2))
    return (start_grad, porosity_grad)
```

```python
import jax
import jax.numpy as jnp
import numpy as np
from jax import lax
from jax.sharding import PartitionSpec as P

DIR_X = np.array([0, 1, -1, 0, 0, 0, 0, 1, -1, 1, -1, 1, -1, 1, -1, 0, 0, 0, 0])
DIR_Y = np.array([0, 0, 0, 1, -1, 0, 0, 1, 1, -1, -1, 0, 0, 0, 0, 1, -1, 1, -1])
DIR_Z = np.array([0, 0, 0, 0, 0, 1, -1, 0, 0, 0, 0, 1, 1, -1, -1, 1, 1, -1, -1])
WEIGHTS = np.array([1.0 / 3.0] + [1.0 / 18.0] * 6 + [1.0 / 36.0] * 12)
RELAX_RATE = 0.8
HI = lax.Precision.HIGHEST


def column(values):
    return np.asarray(values, np.float32)[:, None, None, None]


def collide(field, solid):
    density = jnp.sum(field, axis=0)
    inverse = (1.0 - solid) / density
    vel_x = jnp.sum(field * column(DIR_X), axis=0) * inverse
    vel_y = jnp.sum(field * column(DIR_Y), axis=0) * inverse
    vel_z = jnp.sum(field * column(DIR_Z), axis=0) * inverse
    along = column(DIR_X) * vel_x + column(DIR_Y) * vel_y + column(DIR_Z) * vel_z
    square = vel_x * vel_x + vel_y * vel_y + vel_z * vel_z
    balance = column(WEIGHTS) * density * (1.0 + 3.0 * along + 4.5 * along * along - 1.5 * square)
    return field - RELAX_RATE * (field - balance)


def pull(padded, sign):
    height = padded.shape[2] - 2
    width = padded.shape[3] - 2
    moved = []
    for lane in range(19):
        row_start = 1 - sign * int(DIR_Y[lane])
        col_start = 1 - sign * int(DIR_X[lane])
        piece = padded[lane, :, row_start : row_start + height, col_start : col_start + width]
        moved.append(jnp.roll(piece, sign * int(DIR_Z[lane]), axis=0))
    return jnp.stack(moved)


def one_hot(rows, width, lanes):
    table = np.zeros((rows, width), np.float32)
    for k, lane in enumerate(lanes):
        table[k, lane] = 1.0
    return table


def exchange(fields):
    nx = lax.axis_size("gx")
    ny = lax.axis_size("gy")
    count = len(fields)
    q, layers, height, width = fields[0].shape
    rows = q * layers * height
    pick = jnp.asarray(one_hot(2, width, (0, width - 1)))
    packed = [
        jnp.einsum("kx,nx->kn", pick, g.reshape(rows, width), precision=HI,
                   preferred_element_type=jnp.float32)
        for g in fields
    ]
    first_col = jnp.stack([p[0] for p in packed])
    last_col = jnp.stack([p[1] for p in packed])
    first_row = jnp.stack([g[:, :, 0, :] for g in fields])
    last_row = jnp.stack([g[:, :, height - 1, :] for g in fields])
    cols3 = [p.reshape(2, q, layers, height) for p in packed]
    c00 = jnp.stack([c[0, :, :, 0] for c in cols3])
    c0l = jnp.stack([c[1, :, :, 0] for c in cols3])
    cl0 = jnp.stack([c[0, :, :, height - 1] for c in cols3])
    cll = jnp.stack([c[1, :, :, height - 1] for c in cols3])

    def lin(i, j):
        return i * ny + j

    def shift_x(value, step):
        return lax.ppermute(value, "gx", [(i, (i + step) % nx) for i in range(nx)])

    def shift_y(value, step):
        return lax.ppermute(value, "gy", [(j, (j + step) % ny) for j in range(ny)])

    def shift_xy(value, sx, sy):
        pairs = [(lin(i, j), lin((i + sx) % nx, (j + sy) % ny)) for i in range(nx) for j in range(ny)]
        return lax.ppermute(value, ("gx", "gy"), pairs)

    before_x = shift_x(last_col, 1)
    after_x = shift_x(first_col, -1)
    before_y = shift_y(last_row, 1)
    after_y = shift_y(first_row, -1)
    corner_bb = shift_xy(cll, 1, 1)
    corner_ba = shift_xy(cl0, -1, 1)
    corner_ab = shift_xy(c0l, 1, -1)
    corner_aa = shift_xy(c00, -1, -1)

    place = jnp.asarray(one_hot(2, width + 2, (0, width + 1)))
    out = []
    for n, g in enumerate(fields):
        halo_cols = jnp.stack([before_x[n], after_x[n]])
        sides = jnp.einsum("kn,kx->nx", halo_cols, place, precision=HI,
                           preferred_element_type=jnp.float32).reshape(q, layers, height, width + 2)
        middle = jnp.pad(g, ((0, 0), (0, 0), (0, 0), (1, 1))) + sides
        top = jnp.concatenate(
            [corner_bb[n][:, :, None], before_y[n], corner_ba[n][:, :, None]], axis=2
        )[:, :, None, :]
        bottom = jnp.concatenate(
            [corner_ab[n][:, :, None], after_y[n], corner_aa[n][:, :, None]], axis=2
        )[:, :, None, :]
        out.append(jnp.concatenate([top, middle, bottom], axis=2))
    return out


def on_device(f_start, cotangent, porosity, brick_ids, brick_slot):
    layers_dev = f_start.shape[1]
    rows_dev = f_start.shape[2]
    cols_dev = f_start.shape[3]
    tile_count = cols_dev // 128
    brick_count = layers_dev * rows_dev * tile_count
    listed = brick_ids.reshape(-1)
    slots_of = brick_slot.reshape(-1)
    slot_table = porosity.reshape(-1)
    brick_hit = (listed[:, None] == jnp.arange(brick_count, dtype=jnp.int32)[None, :]).astype(
        jnp.float32
    )
    slot_hit = (
        slots_of[:, None] == jnp.arange(slot_table.shape[0], dtype=jnp.int32)[None, :]
    ).astype(jnp.float32)
    brick_value = jnp.sum(slot_hit * slot_table[None, :], axis=1)
    tile_value = jnp.sum(brick_hit * brick_value[:, None], axis=0)
    solid = jnp.broadcast_to(
        tile_value.reshape(layers_dev, rows_dev, tile_count, 1),
        (layers_dev, rows_dev, tile_count, 128),
    ).reshape(layers_dev, rows_dev, cols_dev)
    back_last = cotangent.astype(jnp.float32)
    collided, cot_ext = exchange([collide(f_start, solid), back_last])
    after_one = pull(collided, 1)
    back_two = pull(cot_ext, -1)
    ignored, undo_two = jax.vjp(collide, after_one, solid)
    back_one, solid_bar_two = undo_two(back_two)
    (back_one_ext,) = exchange([back_one])
    back_one_pulled = pull(back_one_ext, -1)
    ignored_first, undo_one = jax.vjp(collide, f_start, solid)
    start_grad, solid_bar_one = undo_one(back_one_pulled)
    solid_bar = solid_bar_one + solid_bar_two
    tile_sums = jnp.sum(solid_bar.reshape(brick_count, 128), axis=1)
    brick_sum = jnp.sum(brick_hit * tile_sums[None, :], axis=1)
    slot_grad = jnp.sum(slot_hit * brick_sum[:, None], axis=0)
    return (start_grad, slot_grad.reshape(porosity.shape))


def solution(mesh):
    return jax.shard_map(
        on_device,
        mesh=mesh,
        in_specs=(
            P(None, None, "gy", "gx"),
            P(None, None, "gy", "gx"),
            P("gx", "gy", None),
            P("gx", "gy", None),
            P("gx", "gy", None),
        ),
        out_specs=(P(None, None, "gy", "gx"), P("gx", "gy", None)),
        check_vma=False,
    )
```

```python
import jax
import jax.numpy as jnp
import numpy as np
from jax import lax
from jax.sharding import PartitionSpec as P

DIR_X = np.array([0, 1, -1, 0, 0, 0, 0, 1, -1, 1, -1, 1, -1, 1, -1, 0, 0, 0, 0])
DIR_Y = np.array([0, 0, 0, 1, -1, 0, 0, 1, 1, -1, -1, 0, 0, 0, 0, 1, -1, 1, -1])
DIR_Z = np.array([0, 0, 0, 0, 0, 1, -1, 0, 0, 0, 0, 1, 1, -1, -1, 1, 1, -1, -1])
WEIGHTS = np.array([1.0 / 3.0] + [1.0 / 18.0] * 6 + [1.0 / 36.0] * 12)
RELAX_RATE = 0.8
HI = lax.Precision.HIGHEST


def column(values):
    return np.asarray(values, np.float32)[:, None, None, None]


def collide(field, solid):
    density = jnp.sum(field, axis=0)
    inverse = (1.0 - solid) / density
    vel_x = jnp.sum(field * column(DIR_X), axis=0) * inverse
    vel_y = jnp.sum(field * column(DIR_Y), axis=0) * inverse
    vel_z = jnp.sum(field * column(DIR_Z), axis=0) * inverse
    along = column(DIR_X) * vel_x + column(DIR_Y) * vel_y + column(DIR_Z) * vel_z
    square = vel_x * vel_x + vel_y * vel_y + vel_z * vel_z
    balance = column(WEIGHTS) * density * (1.0 + 3.0 * along + 4.5 * along * along - 1.5 * square)
    return field - RELAX_RATE * (field - balance)


def pull(padded, sign):
    height = padded.shape[2] - 2
    width = padded.shape[3] - 2
    moved = []
    for lane in range(19):
        row_start = 1 - sign * int(DIR_Y[lane])
        col_start = 1 - sign * int(DIR_X[lane])
        piece = padded[lane, :, row_start : row_start + height, col_start : col_start + width]
        moved.append(jnp.roll(piece, sign * int(DIR_Z[lane]), axis=0))
    return jnp.stack(moved)


def one_hot(rows, width, lanes):
    table = np.zeros((rows, width), np.float32)
    for k, lane in enumerate(lanes):
        table[k, lane] = 1.0
    return table


def exchange(fields):
    nx = lax.axis_size("gx")
    ny = lax.axis_size("gy")
    height, width = fields[0].shape[2], fields[0].shape[3]
    pick = jnp.asarray(one_hot(4, width, (0, 1, width - 2, width - 1)))
    place = jnp.asarray(one_hot(4, width + 4, (0, 1, width + 2, width + 3)))

    def shift(value, axis, size, step):
        return lax.ppermute(value, axis, [(i, (i + step) % size) for i in range(size)])

    packs = []
    for g in fields:
        b, layers = g.shape[0], g.shape[1]
        packs.append(
            jnp.einsum("kx,nx->kn", pick, g.reshape(b * layers * height, width), precision=HI,
                       preferred_element_type=jnp.float32)
        )
    low = jnp.concatenate([p[0:2] for p in packs], axis=1)
    high = jnp.concatenate([p[2:4] for p in packs], axis=1)
    from_left = shift(high, "gx", nx, 1)
    from_right = shift(low, "gx", nx, -1)

    ext_x = []
    edge_rows_top = []
    edge_rows_bottom = []
    offset = 0
    for g in fields:
        b, layers = g.shape[0], g.shape[1]
        rows = b * layers * height
        halo = jnp.concatenate(
            [from_left[:, offset : offset + rows], from_right[:, offset : offset + rows]], axis=0
        )
        offset += rows
        sides = jnp.einsum("kn,kx->nx", halo, place, precision=HI,
                           preferred_element_type=jnp.float32).reshape(b, layers, height, width + 4)
        padded = jnp.pad(g.astype(jnp.float32), ((0, 0), (0, 0), (0, 0), (2, 2)))
        ext_x.append(padded + sides)
        halo_rows = halo.reshape(4, b, layers, height)
        for chosen, keep in ((slice(0, 2), edge_rows_top), (slice(height - 2, height), edge_rows_bottom)):
            side_rows = jnp.einsum("kbzy,kx->bzyx", halo_rows[:, :, :, chosen], place, precision=HI,
                                   preferred_element_type=jnp.float32)
            keep.append(padded[:, :, chosen, :] + side_rows)
    top = jnp.concatenate(edge_rows_top, axis=0)
    bottom = jnp.concatenate(edge_rows_bottom, axis=0)
    from_up = shift(bottom, "gy", ny, 1)
    from_down = shift(top, "gy", ny, -1)
    out = []
    offset = 0
    for e in ext_x:
        b = e.shape[0]
        out.append(
            jnp.concatenate([from_up[offset : offset + b], e, from_down[offset : offset + b]], axis=2)
        )
        offset += b
    return out


def on_device(f_start, cotangent, porosity, brick_ids, brick_slot):
    layers_dev = f_start.shape[1]
    rows_dev = f_start.shape[2]
    cols_dev = f_start.shape[3]
    tile_count = cols_dev // 128
    brick_count = layers_dev * rows_dev * tile_count
    listed = brick_ids.reshape(-1)
    slots_of = brick_slot.reshape(-1)
    slot_table = porosity.reshape(-1)
    brick_hit = (listed[:, None] == jnp.arange(brick_count, dtype=jnp.int32)[None, :]).astype(
        jnp.float32
    )
    slot_hit = (
        slots_of[:, None] == jnp.arange(slot_table.shape[0], dtype=jnp.int32)[None, :]
    ).astype(jnp.float32)
    brick_value = jnp.sum(slot_hit * slot_table[None, :], axis=1)
    tile_value = jnp.sum(brick_hit * brick_value[:, None], axis=0)
    solid = jnp.broadcast_to(
        tile_value.reshape(layers_dev, rows_dev, tile_count, 1),
        (layers_dev, rows_dev, tile_count, 128),
    ).reshape(layers_dev, rows_dev, cols_dev)
    back_last = cotangent.astype(jnp.float32)
    f_ext, cot_ext, solid_ext = exchange([f_start, back_last, solid[None]])
    solid_ext = solid_ext[0]
    after_one = pull(collide(f_ext, solid_ext), 1)
    back_two = pull(cot_ext, -1)
    ignored, undo_two = jax.vjp(collide, after_one, solid_ext[:, 1:-1, 1:-1])
    back_one, solid_bar_ring = undo_two(back_two)
    back_one_pulled = pull(back_one, -1)
    ignored_first, undo_one = jax.vjp(collide, f_start, solid)
    start_grad, solid_bar_one = undo_one(back_one_pulled)
    solid_bar_two = solid_bar_ring[:, 1:-1, 1:-1]
    solid_bar = solid_bar_one + solid_bar_two
    tile_sums = jnp.sum(solid_bar.reshape(brick_count, 128), axis=1)
    brick_sum = jnp.sum(brick_hit * tile_sums[None, :], axis=1)
    slot_grad = jnp.sum(slot_hit * brick_sum[:, None], axis=0)
    return (start_grad, slot_grad.reshape(porosity.shape))


def solution(mesh):
    return jax.shard_map(
        on_device,
        mesh=mesh,
        in_specs=(
            P(None, None, "gy", "gx"),
            P(None, None, "gy", "gx"),
            P("gx", "gy", None),
            P("gx", "gy", None),
            P("gx", "gy", None),
        ),
        out_specs=(P(None, None, "gy", "gx"), P("gx", "gy", None)),
        check_vma=False,
    )
```

```python
import jax
import jax.numpy as jnp
import numpy as np
from jax import lax
from jax.experimental import pallas as pl
from jax.experimental.pallas import tpu as pltpu
from jax.sharding import PartitionSpec as P

DIR_X = np.array([0, 1, -1, 0, 0, 0, 0, 1, -1, 1, -1, 1, -1, 1, -1, 0, 0, 0, 0])
DIR_Y = np.array([0, 0, 0, 1, -1, 0, 0, 1, 1, -1, -1, 0, 0, 0, 0, 1, -1, 1, -1])
DIR_Z = np.array([0, 0, 0, 0, 0, 1, -1, 0, 0, 0, 0, 1, 1, -1, -1, 1, 1, -1, -1])
WEIGHTS = np.array([1.0 / 3.0] + [1.0 / 18.0] * 6 + [1.0 / 36.0] * 12)
RELAX_RATE = 0.8

ROWS = 48
LANES = 256
TOP = 8


def collide(fields, solid):
    density = fields[0]
    for value in fields[1:]:
        density = density + value
    inverse = (1.0 - solid) / density
    moments = []
    for direction in (DIR_X, DIR_Y, DIR_Z):
        total = None
        for q in range(19):
            if direction[q] == 0:
                continue
            term = fields[q] if direction[q] > 0 else -fields[q]
            total = term if total is None else total + term
        moments.append(total * inverse)
    vel_x, vel_y, vel_z = moments
    square = vel_x * vel_x + vel_y * vel_y + vel_z * vel_z
    out = []
    for q in range(19):
        along = None
        for sign, vel in ((DIR_X[q], vel_x), (DIR_Y[q], vel_y), (DIR_Z[q], vel_z)):
            if sign == 0:
                continue
            term = vel if sign > 0 else -vel
            along = term if along is None else along + term
        if along is None:
            shape = 1.0 - 1.5 * square
        else:
            shape = 1.0 + 3.0 * along + 4.5 * along * along - 1.5 * square
        balance = float(WEIGHTS[q]) * density * shape
        out.append(fields[q] - RELAX_RATE * (fields[q] - balance))
    return out


def plane_list(q_count, layers):
    planes = [(0, q, z) for q in range(q_count) for z in range(layers)]
    planes += [(1, q, z) for q in range(q_count) for z in range(layers)]
    planes += [(2, 0, z) for z in range(layers)]
    return planes


def pack_kernel(f_ref, cot_ref, solid_ref, up_ref, dn_ref, to_right_ref, to_left_ref, tile_ref):
    q_count, layers, height, width = f_ref.shape
    lane = lax.broadcasted_iota(jnp.int32, (ROWS, width), 1)
    to_right_ref[...] = jnp.zeros(to_right_ref.shape, jnp.float32)
    to_left_ref[...] = jnp.zeros(to_left_ref.shape, jnp.float32)
    tile_ref[...] = jnp.zeros(tile_ref.shape, jnp.float32)
    for index, (field, q, z) in enumerate(plane_list(q_count, layers)):
        if field == 0:
            own = f_ref[q, z]
        elif field == 1:
            own = cot_ref[q, z].astype(jnp.float32)
        else:
            own = solid_ref[z]
        row_index = field * q_count + q
        tile_ref[TOP : TOP + height, :] = own
        tile_ref[TOP - 2 : TOP, :] = up_ref[row_index, z]
        tile_ref[TOP + height : TOP + height + 2, :] = dn_ref[row_index, z]
        tile = tile_ref[...]
        group, slot = divmod(index, width // 2)
        mine = (lane == 2 * slot) | (lane == 2 * slot + 1)
        moved = pltpu.roll(tile, (2 * slot - (width - 2)) % width, 1)
        to_right_ref[group] = jnp.where(mine, moved, to_right_ref[group])
        moved = pltpu.roll(tile, (2 * slot) % width, 1)
        to_left_ref[group] = jnp.where(mine, moved, to_left_ref[group])


def compute_kernel(f_ref, cot_ref, solid_ref, up_ref, dn_ref, from_left_ref, from_right_ref,
                   grad_ref, sbar_ref, ef, ec, es, cf, bo, sb2):
    q_count, layers, height, width = f_ref.shape
    lane = lax.broadcasted_iota(jnp.int32, (ROWS, width), 1)
    low_lanes = lane < 2
    high_lanes = lane >= width - 2
    tail = ROWS - (TOP + height + 2)

    def place(target, index, own, up_rows, dn_rows):
        group, slot = divmod(index, width // 2)
        from_r = pltpu.roll(from_right_ref[group], (-2 * slot) % width, 1)
        from_l = pltpu.roll(from_left_ref[group], (width - 2 - 2 * slot) % width, 1)
        target[:, width:LANES] = jnp.where(low_lanes, from_r, jnp.where(high_lanes, from_l, 0.0))
        target[0 : TOP - 2, 0:width] = jnp.zeros((TOP - 2, width), jnp.float32)
        target[TOP + height + 2 : ROWS, 0:width] = jnp.zeros((tail, width), jnp.float32)
        target[TOP - 2 : TOP, 0:width] = up_rows
        target[TOP : TOP + height, 0:width] = own
        target[TOP + height : TOP + height + 2, 0:width] = dn_rows

    for index, (field, q, z) in enumerate(plane_list(q_count, layers)):
        row_index = field * q_count + q
        if field == 0:
            place(ef.at[q, z], index, f_ref[q, z], up_ref[row_index, z], dn_ref[row_index, z])
        elif field == 1:
            place(ec.at[q, z], index, cot_ref[q, z].astype(jnp.float32), up_ref[row_index, z],
                  dn_ref[row_index, z])
        else:
            place(es.at[z], index, solid_ref[z], up_ref[row_index, z], dn_ref[row_index, z])

    def phase_one(z, carry):
        for k in range(ROWS // 8):
            rows = pl.ds(8 * k, 8)
            out = collide([ef[q, z, rows, :] for q in range(q_count)], es[z, rows, :])
            for q in range(q_count):
                cf[q, z, rows, :] = out[q]
        return carry

    lax.fori_loop(0, layers, phase_one, 0)

    def phase_two(z, carry):
        for k in range((ROWS - 8) // 8):
            start = TOP - 1 + 8 * k
            moved = []
            back = []
            for q in range(q_count):
                ex, ey, ez = int(DIR_X[q]), int(DIR_Y[q]), int(DIR_Z[q])
                src = cf[q, (z - ez + layers) % layers, pl.ds(start - ey, 8), :]
                moved.append(pltpu.roll(src, ex % LANES, 1) if ex else src)
                src = ec[q, (z + ez) % layers, pl.ds(start + ey, 8), :]
                back.append(pltpu.roll(src, (-ex) % LANES, 1) if ex else src)
            ignored, undo = jax.vjp(collide, moved, es[z, pl.ds(start, 8), :])
            grad_field, grad_solid = undo(back)
            for q in range(q_count):
                bo[q, z, pl.ds(8 * k, 8), :] = grad_field[q]
            sb2[z, pl.ds(8 * k, 8), :] = grad_solid
        return carry

    lax.fori_loop(0, layers, phase_two, 0)

    def phase_three(z, carry):
        for k in range(height // 8):
            rows = pl.ds(8 * k, 8)
            pulled = []
            for q in range(q_count):
                ex, ey, ez = int(DIR_X[q]), int(DIR_Y[q]), int(DIR_Z[q])
                src = bo[q, (z + ez) % layers, pl.ds(1 + ey + 8 * k, 8), :]
                if ex:
                    src = pltpu.roll(src, (-ex) % LANES, 1)
                pulled.append(src[:, 0:width])
            field = [f_ref[q, z, rows, :] for q in range(q_count)]
            ignored, undo = jax.vjp(collide, field, solid_ref[z, rows, :])
            grad_field, grad_solid = undo(pulled)
            for q in range(q_count):
                grad_ref[q, z, rows, :] = grad_field[q]
            sbar_ref[z, rows, :] = grad_solid + sb2[z, pl.ds(1 + 8 * k, 8), 0:width]
        return carry

    lax.fori_loop(0, layers, phase_three, 0)


def vmem_specs(count):
    return [pl.BlockSpec(memory_space=pltpu.VMEM) for _ in range(count)]


def on_device(f_start, cotangent, porosity, brick_ids, brick_slot):
    q_count, layers_dev, rows_dev, cols_dev = f_start.shape
    nx = lax.axis_size("gx")
    ny = lax.axis_size("gy")
    tile_count = cols_dev // 128
    brick_count = layers_dev * rows_dev * tile_count
    listed = brick_ids.reshape(-1)
    slots_of = brick_slot.reshape(-1)
    slot_table = porosity.reshape(-1)
    brick_hit = (listed[:, None] == jnp.arange(brick_count, dtype=jnp.int32)[None, :]).astype(
        jnp.float32
    )
    slot_hit = (
        slots_of[:, None] == jnp.arange(slot_table.shape[0], dtype=jnp.int32)[None, :]
    ).astype(jnp.float32)
    brick_value = jnp.sum(slot_hit * slot_table[None, :], axis=1)
    tile_value = jnp.sum(brick_hit * brick_value[:, None], axis=0)
    solid = jnp.broadcast_to(
        tile_value.reshape(layers_dev, rows_dev, tile_count, 1),
        (layers_dev, rows_dev, tile_count, 128),
    ).reshape(layers_dev, rows_dev, cols_dev)

    def shift(value, axis, size, step):
        return lax.ppermute(value, axis, [(i, (i + step) % size) for i in range(size)])

    cot32 = cotangent.astype(jnp.float32)
    first_rows = jnp.concatenate([f_start[:, :, 0:2], cot32[:, :, 0:2], solid[None, :, 0:2]], axis=0)
    last_rows = jnp.concatenate(
        [f_start[:, :, rows_dev - 2 :], cot32[:, :, rows_dev - 2 :], solid[None, :, rows_dev - 2 :]],
        axis=0,
    )
    up_rows = shift(last_rows, "gy", ny, 1)
    dn_rows = shift(first_rows, "gy", ny, -1)
    plane_count = (2 * q_count + 1) * layers_dev
    groups = -(-plane_count // (cols_dev // 2))
    buffer = jax.ShapeDtypeStruct((groups, ROWS, cols_dev), jnp.float32)
    to_right, to_left = pl.pallas_call(
        pack_kernel,
        out_shape=(buffer, buffer),
        in_specs=vmem_specs(5),
        out_specs=tuple(vmem_specs(2)),
        scratch_shapes=[pltpu.VMEM((ROWS, cols_dev), jnp.float32)],
    )(f_start, cotangent, solid, up_rows, dn_rows)
    from_left = shift(to_right, "gx", nx, 1)
    from_right = shift(to_left, "gx", nx, -1)
    big = pltpu.VMEM((q_count, layers_dev, ROWS, LANES), jnp.float32)
    start_grad, solid_bar = pl.pallas_call(
        compute_kernel,
        out_shape=(
            jax.ShapeDtypeStruct(f_start.shape, jnp.float32),
            jax.ShapeDtypeStruct(solid.shape, jnp.float32),
        ),
        in_specs=vmem_specs(7),
        out_specs=tuple(vmem_specs(2)),
        scratch_shapes=[
            big,
            big,
            pltpu.VMEM((layers_dev, ROWS, LANES), jnp.float32),
            big,
            pltpu.VMEM((q_count, layers_dev, ROWS - 8, LANES), jnp.float32),
            pltpu.VMEM((layers_dev, ROWS - 8, LANES), jnp.float32),
        ],
        compiler_params=pltpu.CompilerParams(vmem_limit_bytes=48 * 1024 * 1024),
    )(f_start, cotangent, solid, up_rows, dn_rows, from_left, from_right)
    tile_sums = jnp.sum(solid_bar.reshape(brick_count, 128), axis=1)
    brick_sum = jnp.sum(brick_hit * tile_sums[None, :], axis=1)
    slot_grad = jnp.sum(slot_hit * brick_sum[:, None], axis=0)
    return (start_grad, slot_grad.reshape(porosity.shape))


def solution(mesh):
    return jax.shard_map(
        on_device,
        mesh=mesh,
        in_specs=(
            P(None, None, "gy", "gx"),
            P(None, None, "gy", "gx"),
            P("gx", "gy", None),
            P("gx", "gy", None),
            P("gx", "gy", None),
        ),
        out_specs=(P(None, None, "gy", "gx"), P("gx", "gy", None)),
        check_vma=False,
    )
```

```python
import jax
import jax.numpy as jnp
import numpy as np
from jax import lax
from jax.experimental import pallas as pl
from jax.experimental.pallas import tpu as pltpu
from jax.sharding import PartitionSpec as P

DIR_X = np.array([0, 1, -1, 0, 0, 0, 0, 1, -1, 1, -1, 1, -1, 1, -1, 0, 0, 0, 0])
DIR_Y = np.array([0, 0, 0, 1, -1, 0, 0, 1, 1, -1, -1, 0, 0, 0, 0, 1, -1, 1, -1])
DIR_Z = np.array([0, 0, 0, 0, 0, 1, -1, 0, 0, 0, 0, 1, 1, -1, -1, 1, 1, -1, -1])
WEIGHTS = np.array([1.0 / 3.0] + [1.0 / 18.0] * 6 + [1.0 / 36.0] * 12)
RELAX_RATE = 0.8

ROWS = 48
LANES = 256
TOP = 2


def collide(fields, solid):
    density = fields[0]
    for value in fields[1:]:
        density = density + value
    inverse = (1.0 - solid) / density
    moments = []
    for direction in (DIR_X, DIR_Y, DIR_Z):
        total = None
        for q in range(19):
            if direction[q] == 0:
                continue
            term = fields[q] if direction[q] > 0 else -fields[q]
            total = term if total is None else total + term
        moments.append(total * inverse)
    vel_x, vel_y, vel_z = moments
    square = vel_x * vel_x + vel_y * vel_y + vel_z * vel_z
    out = []
    for q in range(19):
        along = None
        for sign, vel in ((DIR_X[q], vel_x), (DIR_Y[q], vel_y), (DIR_Z[q], vel_z)):
            if sign == 0:
                continue
            term = vel if sign > 0 else -vel
            along = term if along is None else along + term
        if along is None:
            shape = 1.0 - 1.5 * square
        else:
            shape = 1.0 + 3.0 * along + 4.5 * along * along - 1.5 * square
        balance = float(WEIGHTS[q]) * density * shape
        out.append(fields[q] - RELAX_RATE * (fields[q] - balance))
    return out


def plane_list(q_count, layers):
    planes = [(0, q, z) for q in range(q_count) for z in range(layers)]
    planes += [(1, q, z) for q in range(q_count) for z in range(layers)]
    planes += [(2, 0, z) for z in range(layers)]
    return planes


def pack_kernel(f_ref, cot_ref, solid_ref, up_ref, dn_ref, to_right_ref, to_left_ref):
    q_count, layers, height, width = f_ref.shape
    groups = to_right_ref.shape[0]
    lane_own = lax.broadcasted_iota(jnp.int32, (height, width), 1)
    lane_edge = lax.broadcasted_iota(jnp.int32, (2, width), 1)
    zero_own = jnp.zeros((height, width), jnp.float32)
    zero_edge = jnp.zeros((2, width), jnp.float32)
    acc = {(side, part, g): (zero_own if part == 1 else zero_edge)
           for side in range(2) for part in range(3) for g in range(groups)}
    for index, (field, q, z) in enumerate(plane_list(q_count, layers)):
        if field == 0:
            own = f_ref[q, z]
        elif field == 1:
            own = cot_ref[q, z].astype(jnp.float32)
        else:
            own = solid_ref[z]
        row_index = field * q_count + q
        parts = (up_ref[row_index, z], own, dn_ref[row_index, z])
        group, slot = divmod(index, width // 2)
        for side, shift in ((0, (2 * slot - (width - 2)) % width), (1, (2 * slot) % width)):
            for part, value in enumerate(parts):
                lane = lane_own if part == 1 else lane_edge
                mine = (lane == 2 * slot) | (lane == 2 * slot + 1)
                key = (side, part, group)
                acc[key] = jnp.where(mine, pltpu.roll(value, shift, 1), acc[key])
    zero_tail = jnp.zeros((ROWS - TOP - height - 2, width), jnp.float32)
    for side, out in ((0, to_right_ref), (1, to_left_ref)):
        for g in range(groups):
            out[g, 0:TOP] = acc[(side, 0, g)]
            out[g, TOP : TOP + height] = acc[(side, 1, g)]
            out[g, TOP + height : TOP + height + 2] = acc[(side, 2, g)]
            out[g, TOP + height + 2 : ROWS] = zero_tail


def compute_kernel(f_ref, cot_ref, solid_ref, up_ref, dn_ref, from_left_ref, from_right_ref,
                   grad_ref, sbar_ref, ef, ec, es, cf, bo, sb2):
    q_count, layers, height, width = f_ref.shape
    lane = lax.broadcasted_iota(jnp.int32, (ROWS, width), 1)
    low_lanes = lane < 2
    high_lanes = lane >= width - 2
    tail = ROWS - (TOP + height + 2)

    def place(target, index, own, up_rows, dn_rows):
        group, slot = divmod(index, width // 2)
        from_r = pltpu.roll(from_right_ref[group], (-2 * slot) % width, 1)
        from_l = pltpu.roll(from_left_ref[group], (width - 2 - 2 * slot) % width, 1)
        target[:, width:LANES] = jnp.where(low_lanes, from_r, jnp.where(high_lanes, from_l, 0.0))
        target[TOP + height + 2 : ROWS, 0:width] = jnp.zeros((tail, width), jnp.float32)
        target[TOP - 2 : TOP, 0:width] = up_rows
        target[TOP : TOP + height, 0:width] = own
        target[TOP + height : TOP + height + 2, 0:width] = dn_rows

    for index, (field, q, z) in enumerate(plane_list(q_count, layers)):
        row_index = field * q_count + q
        if field == 0:
            place(ef.at[q, z], index, f_ref[q, z], up_ref[row_index, z], dn_ref[row_index, z])
        elif field == 1:
            place(ec.at[q, z], index, cot_ref[q, z].astype(jnp.float32), up_ref[row_index, z],
                  dn_ref[row_index, z])
        else:
            place(es.at[z], index, solid_ref[z], up_ref[row_index, z], dn_ref[row_index, z])

    def phase_one(z, carry):
        for k in range((TOP + height + 2 + 7) // 8):
            rows = pl.ds(8 * k, 8)
            out = collide([ef[q, z, rows, :] for q in range(q_count)], es[z, rows, :])
            for q in range(q_count):
                cf[q, z, rows, :] = out[q]
        return carry

    lax.fori_loop(0, layers, phase_one, 0)

    def phase_two(z, carry):
        for k in range((ROWS - 8) // 8):
            start = TOP - 1 + 8 * k
            moved = []
            back = []
            for q in range(q_count):
                ex, ey, ez = int(DIR_X[q]), int(DIR_Y[q]), int(DIR_Z[q])
                src = cf[q, (z - ez + layers) % layers, pl.ds(start - ey, 8), :]
                moved.append(pltpu.roll(src, ex % LANES, 1) if ex else src)
                src = ec[q, (z + ez) % layers, pl.ds(start + ey, 8), :]
                back.append(pltpu.roll(src, (-ex) % LANES, 1) if ex else src)
            ignored, undo = jax.vjp(collide, moved, es[z, pl.ds(start, 8), :])
            grad_field, grad_solid = undo(back)
            for q in range(q_count):
                bo[q, z, pl.ds(8 * k, 8), :] = grad_field[q]
            sb2[z, pl.ds(8 * k, 8), :] = grad_solid
        return carry

    lax.fori_loop(0, layers, phase_two, 0)

    def phase_three(z, carry):
        for k in range(height // 8):
            rows = pl.ds(8 * k, 8)
            pulled = []
            for q in range(q_count):
                ex, ey, ez = int(DIR_X[q]), int(DIR_Y[q]), int(DIR_Z[q])
                src = bo[q, (z + ez) % layers, pl.ds(1 + ey + 8 * k, 8), :]
                if ex:
                    src = pltpu.roll(src, (-ex) % LANES, 1)
                pulled.append(src[:, 0:width])
            field = [f_ref[q, z, rows, :] for q in range(q_count)]
            ignored, undo = jax.vjp(collide, field, solid_ref[z, rows, :])
            grad_field, grad_solid = undo(pulled)
            for q in range(q_count):
                grad_ref[q, z, rows, :] = grad_field[q]
            sbar_ref[z, rows, :] = grad_solid + sb2[z, pl.ds(1 + 8 * k, 8), 0:width]
        return carry

    lax.fori_loop(0, layers, phase_three, 0)


def vmem_specs(count):
    return [pl.BlockSpec(memory_space=pltpu.VMEM) for _ in range(count)]


def on_device(f_start, cotangent, porosity, brick_ids, brick_slot):
    q_count, layers_dev, rows_dev, cols_dev = f_start.shape
    nx = lax.axis_size("gx")
    ny = lax.axis_size("gy")
    tile_count = cols_dev // 128
    brick_count = layers_dev * rows_dev * tile_count
    listed = brick_ids.reshape(-1)
    slots_of = brick_slot.reshape(-1)
    slot_table = porosity.reshape(-1)
    brick_hit = (listed[:, None] == jnp.arange(brick_count, dtype=jnp.int32)[None, :]).astype(
        jnp.float32
    )
    slot_hit = (
        slots_of[:, None] == jnp.arange(slot_table.shape[0], dtype=jnp.int32)[None, :]
    ).astype(jnp.float32)
    brick_value = jnp.sum(slot_hit * slot_table[None, :], axis=1)
    tile_value = jnp.sum(brick_hit * brick_value[:, None], axis=0)
    solid = jnp.broadcast_to(
        tile_value.reshape(layers_dev, rows_dev, tile_count, 1),
        (layers_dev, rows_dev, tile_count, 128),
    ).reshape(layers_dev, rows_dev, cols_dev)

    def shift(value, axis, size, step):
        return lax.ppermute(value, axis, [(i, (i + step) % size) for i in range(size)])

    cot32 = cotangent.astype(jnp.float32)
    first_rows = jnp.concatenate([f_start[:, :, 0:2], cot32[:, :, 0:2], solid[None, :, 0:2]], axis=0)
    last_rows = jnp.concatenate(
        [f_start[:, :, rows_dev - 2 :], cot32[:, :, rows_dev - 2 :], solid[None, :, rows_dev - 2 :]],
        axis=0,
    )
    up_rows = shift(last_rows, "gy", ny, 1)
    dn_rows = shift(first_rows, "gy", ny, -1)
    plane_count = (2 * q_count + 1) * layers_dev
    groups = -(-plane_count // (cols_dev // 2))
    buffer = jax.ShapeDtypeStruct((groups, ROWS, cols_dev), jnp.float32)
    to_right, to_left = pl.pallas_call(
        pack_kernel,
        out_shape=(buffer, buffer),
        in_specs=vmem_specs(5),
        out_specs=tuple(vmem_specs(2)),
    )(f_start, cotangent, solid, up_rows, dn_rows)
    from_left = shift(to_right, "gx", nx, 1)
    from_right = shift(to_left, "gx", nx, -1)
    big = pltpu.VMEM((q_count, layers_dev, ROWS, LANES), jnp.float32)
    start_grad, solid_bar = pl.pallas_call(
        compute_kernel,
        out_shape=(
            jax.ShapeDtypeStruct(f_start.shape, jnp.float32),
            jax.ShapeDtypeStruct(solid.shape, jnp.float32),
        ),
        in_specs=vmem_specs(7),
        out_specs=tuple(vmem_specs(2)),
        scratch_shapes=[
            big,
            big,
            pltpu.VMEM((layers_dev, ROWS, LANES), jnp.float32),
            big,
            pltpu.VMEM((q_count, layers_dev, ROWS - 8, LANES), jnp.float32),
            pltpu.VMEM((layers_dev, ROWS - 8, LANES), jnp.float32),
        ],
        compiler_params=pltpu.CompilerParams(vmem_limit_bytes=48 * 1024 * 1024),
    )(f_start, cotangent, solid, up_rows, dn_rows, from_left, from_right)
    tile_sums = jnp.sum(solid_bar.reshape(brick_count, 128), axis=1)
    brick_sum = jnp.sum(brick_hit * tile_sums[None, :], axis=1)
    slot_grad = jnp.sum(slot_hit * brick_sum[:, None], axis=0)
    return (start_grad, slot_grad.reshape(porosity.shape))


def solution(mesh):
    return jax.shard_map(
        on_device,
        mesh=mesh,
        in_specs=(
            P(None, None, "gy", "gx"),
            P(None, None, "gy", "gx"),
            P("gx", "gy", None),
            P("gx", "gy", None),
            P("gx", "gy", None),
        ),
        out_specs=(P(None, None, "gy", "gx"), P("gx", "gy", None)),
        check_vma=False,
    )
```

```python
import jax
import jax.numpy as jnp
import numpy as np
from jax import lax
from jax.experimental import pallas as pl
from jax.experimental.pallas import tpu as pltpu
from jax.sharding import PartitionSpec as P

DIR_X = np.array([0, 1, -1, 0, 0, 0, 0, 1, -1, 1, -1, 1, -1, 1, -1, 0, 0, 0, 0])
DIR_Y = np.array([0, 0, 0, 1, -1, 0, 0, 1, 1, -1, -1, 0, 0, 0, 0, 1, -1, 1, -1])
DIR_Z = np.array([0, 0, 0, 0, 0, 1, -1, 0, 0, 0, 0, 1, 1, -1, -1, 1, 1, -1, -1])
WEIGHTS = np.array([1.0 / 3.0] + [1.0 / 18.0] * 6 + [1.0 / 36.0] * 12)
RELAX_RATE = 0.8

ROWS = 48
LANES = 256
TOP = 2


def collide(fields, solid):
    density = fields[0]
    for value in fields[1:]:
        density = density + value
    inverse = (1.0 - solid) / density
    moments = []
    for direction in (DIR_X, DIR_Y, DIR_Z):
        total = None
        for q in range(19):
            if direction[q] == 0:
                continue
            term = fields[q] if direction[q] > 0 else -fields[q]
            total = term if total is None else total + term
        moments.append(total * inverse)
    vel_x, vel_y, vel_z = moments
    square = vel_x * vel_x + vel_y * vel_y + vel_z * vel_z
    out = []
    for q in range(19):
        along = None
        for sign, vel in ((DIR_X[q], vel_x), (DIR_Y[q], vel_y), (DIR_Z[q], vel_z)):
            if sign == 0:
                continue
            term = vel if sign > 0 else -vel
            along = term if along is None else along + term
        if along is None:
            shape = 1.0 - 1.5 * square
        else:
            shape = 1.0 + 3.0 * along + 4.5 * along * along - 1.5 * square
        balance = float(WEIGHTS[q]) * density * shape
        out.append(fields[q] - RELAX_RATE * (fields[q] - balance))
    return out


def plane_list(q_count, layers):
    planes = [(0, q, z) for q in range(q_count) for z in range(layers)]
    planes += [(1, q, z) for q in range(q_count) for z in range(layers)]
    planes += [(2, 0, z) for z in range(layers)]
    return planes


def pack_own_kernel(f_ref, cot_ref, solid_ref, to_right_ref, to_left_ref):
    q_count, layers, height, width = f_ref.shape
    groups = to_right_ref.shape[0]
    lane = lax.broadcasted_iota(jnp.int32, (height, width), 1)
    zero = jnp.zeros((height, width), jnp.float32)
    acc = {(side, g): zero for side in range(2) for g in range(groups)}
    for index, (field, q, z) in enumerate(plane_list(q_count, layers)):
        if field == 0:
            own = f_ref[q, z]
        elif field == 1:
            own = cot_ref[q, z].astype(jnp.float32)
        else:
            own = solid_ref[z]
        group, slot = divmod(index, width // 2)
        mine = (lane == 2 * slot) | (lane == 2 * slot + 1)
        for side, shift in ((0, (2 * slot - (width - 2)) % width), (1, (2 * slot) % width)):
            acc[(side, group)] = jnp.where(mine, pltpu.roll(own, shift, 1), acc[(side, group)])
    for side, out in ((0, to_right_ref), (1, to_left_ref)):
        for g in range(groups):
            out[g] = acc[(side, g)]


def pack_edge_kernel(own_right_ref, own_left_ref, up_ref, dn_ref, to_right_ref, to_left_ref):
    groups, height, width = own_right_ref.shape
    planes = plane_list((up_ref.shape[0] - 1) // 2, up_ref.shape[1])
    q_count = (up_ref.shape[0] - 1) // 2
    lane = lax.broadcasted_iota(jnp.int32, (2, width), 1)
    zero = jnp.zeros((2, width), jnp.float32)
    acc = {(side, part, g): zero for side in range(2) for part in range(2) for g in range(groups)}
    for index, (field, q, z) in enumerate(planes):
        row_index = field * q_count + q
        group, slot = divmod(index, width // 2)
        mine = (lane == 2 * slot) | (lane == 2 * slot + 1)
        for side, shift in ((0, (2 * slot - (width - 2)) % width), (1, (2 * slot) % width)):
            for part, value in enumerate((up_ref[row_index, z], dn_ref[row_index, z])):
                key = (side, part, group)
                acc[key] = jnp.where(mine, pltpu.roll(value, shift, 1), acc[key])
    zero_tail = jnp.zeros((ROWS - TOP - height - 2, width), jnp.float32)
    for side, own, out in ((0, own_right_ref, to_right_ref), (1, own_left_ref, to_left_ref)):
        for g in range(groups):
            out[g, 0:TOP] = acc[(side, 0, g)]
            out[g, TOP : TOP + height] = own[g]
            out[g, TOP + height : TOP + height + 2] = acc[(side, 1, g)]
            out[g, TOP + height + 2 : ROWS] = zero_tail


def compute_kernel(f_hbm, cot_hbm, solid_ref, up_ref, dn_ref, from_left_ref, from_right_ref,
                   grad_ref, sbar_ref, ef, ec, es, cf, bo, sb2, f_ref, cot_ref, sems):
    q_count, layers, height, width = f_ref.shape
    f_copy = pltpu.make_async_copy(f_hbm, f_ref, sems.at[0])
    cot_copy = pltpu.make_async_copy(cot_hbm, cot_ref, sems.at[1])
    f_copy.start()
    cot_copy.start()
    lane = lax.broadcasted_iota(jnp.int32, (ROWS, width), 1)
    low_lanes = lane < 2
    high_lanes = lane >= width - 2
    tail = ROWS - (TOP + height + 2)

    def place_halo(target, index, up_rows, dn_rows):
        group, slot = divmod(index, width // 2)
        from_r = pltpu.roll(from_right_ref[group], (-2 * slot) % width, 1)
        from_l = pltpu.roll(from_left_ref[group], (width - 2 - 2 * slot) % width, 1)
        target[:, width:LANES] = jnp.where(low_lanes, from_r, jnp.where(high_lanes, from_l, 0.0))
        target[TOP + height + 2 : ROWS, 0:width] = jnp.zeros((tail, width), jnp.float32)
        target[TOP - 2 : TOP, 0:width] = up_rows
        target[TOP + height : TOP + height + 2, 0:width] = dn_rows

    targets = []
    for index, (field, q, z) in enumerate(plane_list(q_count, layers)):
        row_index = field * q_count + q
        target = (ef.at[q, z], ec.at[q, z], es.at[z])[field]
        place_halo(target, index, up_ref[row_index, z], dn_ref[row_index, z])
        targets.append((field, q, z, target))
    f_copy.wait()
    cot_copy.wait()
    for field, q, z, target in targets:
        if field == 0:
            own = f_ref[q, z]
        elif field == 1:
            own = cot_ref[q, z].astype(jnp.float32)
        else:
            own = solid_ref[z]
        target[TOP : TOP + height, 0:width] = own

    def phase_one(z, carry):
        for k in range((TOP + height + 2 + 7) // 8):
            rows = pl.ds(8 * k, 8)
            out = collide([ef[q, z, rows, :] for q in range(q_count)], es[z, rows, :])
            for q in range(q_count):
                cf[q, z, rows, :] = out[q]
        return carry

    lax.fori_loop(0, layers, phase_one, 0)

    def phase_two(z, carry):
        for k in range((ROWS - 8) // 8):
            start = TOP - 1 + 8 * k
            moved = []
            back = []
            for q in range(q_count):
                ex, ey, ez = int(DIR_X[q]), int(DIR_Y[q]), int(DIR_Z[q])
                src = cf[q, (z - ez + layers) % layers, pl.ds(start - ey, 8), :]
                moved.append(pltpu.roll(src, ex % LANES, 1) if ex else src)
                src = ec[q, (z + ez) % layers, pl.ds(start + ey, 8), :]
                back.append(pltpu.roll(src, (-ex) % LANES, 1) if ex else src)
            ignored, undo = jax.vjp(collide, moved, es[z, pl.ds(start, 8), :])
            grad_field, grad_solid = undo(back)
            for q in range(q_count):
                bo[q, z, pl.ds(8 * k, 8), :] = grad_field[q]
            sb2[z, pl.ds(8 * k, 8), :] = grad_solid
        return carry

    lax.fori_loop(0, layers, phase_two, 0)

    def phase_three(z, carry):
        for k in range(height // 8):
            rows = pl.ds(8 * k, 8)
            pulled = []
            for q in range(q_count):
                ex, ey, ez = int(DIR_X[q]), int(DIR_Y[q]), int(DIR_Z[q])
                src = bo[q, (z + ez) % layers, pl.ds(1 + ey + 8 * k, 8), :]
                if ex:
                    src = pltpu.roll(src, (-ex) % LANES, 1)
                pulled.append(src[:, 0:width])
            field = [f_ref[q, z, rows, :] for q in range(q_count)]
            ignored, undo = jax.vjp(collide, field, solid_ref[z, rows, :])
            grad_field, grad_solid = undo(pulled)
            for q in range(q_count):
                grad_ref[q, z, rows, :] = grad_field[q]
            sbar_ref[z, rows, :] = grad_solid + sb2[z, pl.ds(1 + 8 * k, 8), 0:width]
        return carry

    lax.fori_loop(0, layers, phase_three, 0)


def vmem_specs(count):
    return [pl.BlockSpec(memory_space=pltpu.VMEM) for _ in range(count)]


def on_device(f_start, cotangent, porosity, brick_ids, brick_slot):
    q_count, layers_dev, rows_dev, cols_dev = f_start.shape
    nx = lax.axis_size("gx")
    ny = lax.axis_size("gy")
    tile_count = cols_dev // 128
    brick_count = layers_dev * rows_dev * tile_count
    listed = brick_ids.reshape(-1)
    slots_of = brick_slot.reshape(-1)
    slot_table = porosity.reshape(-1)
    brick_hit = (listed[:, None] == jnp.arange(brick_count, dtype=jnp.int32)[None, :]).astype(
        jnp.float32
    )
    slot_hit = (
        slots_of[:, None] == jnp.arange(slot_table.shape[0], dtype=jnp.int32)[None, :]
    ).astype(jnp.float32)
    brick_value = jnp.sum(slot_hit * slot_table[None, :], axis=1)
    tile_value = jnp.sum(brick_hit * brick_value[:, None], axis=0)
    solid = jnp.broadcast_to(
        tile_value.reshape(layers_dev, rows_dev, tile_count, 1),
        (layers_dev, rows_dev, tile_count, 128),
    ).reshape(layers_dev, rows_dev, cols_dev)

    def shift(value, axis, size, step):
        return lax.ppermute(value, axis, [(i, (i + step) % size) for i in range(size)])

    cot32 = cotangent.astype(jnp.float32)
    first_rows = jnp.concatenate([f_start[:, :, 0:2], cot32[:, :, 0:2], solid[None, :, 0:2]], axis=0)
    last_rows = jnp.concatenate(
        [f_start[:, :, rows_dev - 2 :], cot32[:, :, rows_dev - 2 :], solid[None, :, rows_dev - 2 :]],
        axis=0,
    )
    up_rows = shift(last_rows, "gy", ny, 1)
    dn_rows = shift(first_rows, "gy", ny, -1)
    plane_count = (2 * q_count + 1) * layers_dev
    groups = -(-plane_count // (cols_dev // 2))
    buffer = jax.ShapeDtypeStruct((groups, ROWS, cols_dev), jnp.float32)
    own_buffer = jax.ShapeDtypeStruct((groups, rows_dev, cols_dev), jnp.float32)
    own_right, own_left = pl.pallas_call(
        pack_own_kernel,
        out_shape=(own_buffer, own_buffer),
        in_specs=vmem_specs(3),
        out_specs=tuple(vmem_specs(2)),
    )(f_start, cotangent, solid)
    to_right, to_left = pl.pallas_call(
        pack_edge_kernel,
        out_shape=(buffer, buffer),
        in_specs=vmem_specs(4),
        out_specs=tuple(vmem_specs(2)),
    )(own_right, own_left, up_rows, dn_rows)
    from_left = shift(to_right, "gx", nx, 1)
    from_right = shift(to_left, "gx", nx, -1)
    big = pltpu.VMEM((q_count, layers_dev, ROWS, LANES), jnp.float32)
    start_grad, solid_bar = pl.pallas_call(
        compute_kernel,
        out_shape=(
            jax.ShapeDtypeStruct(f_start.shape, jnp.float32),
            jax.ShapeDtypeStruct(solid.shape, jnp.float32),
        ),
        in_specs=[pl.BlockSpec(memory_space=pl.ANY)] * 2 + vmem_specs(5),
        out_specs=tuple(vmem_specs(2)),
        scratch_shapes=[
            big,
            big,
            pltpu.VMEM((layers_dev, ROWS, LANES), jnp.float32),
            big,
            pltpu.VMEM((q_count, layers_dev, ROWS - 8, LANES), jnp.float32),
            pltpu.VMEM((layers_dev, ROWS - 8, LANES), jnp.float32),
            pltpu.VMEM(f_start.shape, jnp.float32),
            pltpu.VMEM(cotangent.shape, cotangent.dtype),
            pltpu.SemaphoreType.DMA((2,)),
        ],
        compiler_params=pltpu.CompilerParams(vmem_limit_bytes=48 * 1024 * 1024),
    )(f_start, cotangent, solid, up_rows, dn_rows, from_left, from_right)
    tile_sums = jnp.sum(solid_bar.reshape(brick_count, 128), axis=1)
    brick_sum = jnp.sum(brick_hit * tile_sums[None, :], axis=1)
    slot_grad = jnp.sum(slot_hit * brick_sum[:, None], axis=0)
    return (start_grad, slot_grad.reshape(porosity.shape))


def solution(mesh):
    return jax.shard_map(
        on_device,
        mesh=mesh,
        in_specs=(
            P(None, None, "gy", "gx"),
            P(None, None, "gy", "gx"),
            P("gx", "gy", None),
            P("gx", "gy", None),
            P("gx", "gy", None),
        ),
        out_specs=(P(None, None, "gy", "gx"), P("gx", "gy", None)),
        check_vma=False,
    )
```

```python
import jax
import jax.numpy as jnp
import numpy as np
from jax import lax
from jax.experimental import pallas as pl
from jax.experimental.pallas import tpu as pltpu
from jax.sharding import PartitionSpec as P

DIR_X = np.array([0, 1, -1, 0, 0, 0, 0, 1, -1, 1, -1, 1, -1, 1, -1, 0, 0, 0, 0])
DIR_Y = np.array([0, 0, 0, 1, -1, 0, 0, 1, 1, -1, -1, 0, 0, 0, 0, 1, -1, 1, -1])
DIR_Z = np.array([0, 0, 0, 0, 0, 1, -1, 0, 0, 0, 0, 1, 1, -1, -1, 1, 1, -1, -1])
WEIGHTS = np.array([1.0 / 3.0] + [1.0 / 18.0] * 6 + [1.0 / 36.0] * 12)
RELAX_RATE = 0.8

ROWS = 48
LANES = 256
TOP = 2


def collide(fields, solid):
    density = fields[0]
    for value in fields[1:]:
        density = density + value
    inverse = (1.0 - solid) / density
    moments = []
    for direction in (DIR_X, DIR_Y, DIR_Z):
        total = None
        for q in range(19):
            if direction[q] == 0:
                continue
            term = fields[q] if direction[q] > 0 else -fields[q]
            total = term if total is None else total + term
        moments.append(total * inverse)
    vel_x, vel_y, vel_z = moments
    square = vel_x * vel_x + vel_y * vel_y + vel_z * vel_z
    out = []
    for q in range(19):
        along = None
        for sign, vel in ((DIR_X[q], vel_x), (DIR_Y[q], vel_y), (DIR_Z[q], vel_z)):
            if sign == 0:
                continue
            term = vel if sign > 0 else -vel
            along = term if along is None else along + term
        if along is None:
            shape = 1.0 - 1.5 * square
        else:
            shape = 1.0 + 3.0 * along + 4.5 * along * along - 1.5 * square
        balance = float(WEIGHTS[q]) * density * shape
        out.append(fields[q] - RELAX_RATE * (fields[q] - balance))
    return out


def plane_list(q_count, layers):
    planes = [(0, q, z) for q in range(q_count) for z in range(layers)]
    planes += [(1, q, z) for q in range(q_count) for z in range(layers)]
    planes += [(2, 0, z) for z in range(layers)]
    return planes


def pack_own_kernel(f_ref, cot_ref, solid_ref, to_right_ref, to_left_ref):
    q_count, layers, height, width = f_ref.shape
    groups = to_right_ref.shape[0]
    lane = lax.broadcasted_iota(jnp.int32, (height, width), 1)
    zero = jnp.zeros((height, width), jnp.float32)
    acc = {(side, g): zero for side in range(2) for g in range(groups)}
    for index, (field, q, z) in enumerate(plane_list(q_count, layers)):
        if field == 0:
            own = f_ref[q, z]
        elif field == 1:
            own = cot_ref[q, z].astype(jnp.float32)
        else:
            own = solid_ref[z]
        group, slot = divmod(index, width // 2)
        mine = (lane == 2 * slot) | (lane == 2 * slot + 1)
        for side, shift in ((0, (2 * slot - (width - 2)) % width), (1, (2 * slot) % width)):
            acc[(side, group)] = jnp.where(mine, pltpu.roll(own, shift, 1), acc[(side, group)])
    for side, out in ((0, to_right_ref), (1, to_left_ref)):
        for g in range(groups):
            out[g] = acc[(side, g)]


def pack_edge_kernel(own_right_ref, own_left_ref, up_hbm, dn_hbm, to_right_ref, to_left_ref, up_ref, dn_ref,
                     sems):
    groups, height, width = own_right_ref.shape
    up_copy = pltpu.make_async_copy(up_hbm, up_ref, sems.at[0])
    dn_copy = pltpu.make_async_copy(dn_hbm, dn_ref, sems.at[1])
    up_copy.start()
    dn_copy.start()
    up_copy.wait()
    dn_copy.wait()
    planes = plane_list((up_ref.shape[0] - 1) // 2, up_ref.shape[1] // 2)
    q_count = (up_ref.shape[0] - 1) // 2
    lane = lax.broadcasted_iota(jnp.int32, (2, width), 1)
    zero = jnp.zeros((2, width), jnp.float32)
    acc = {(side, part, g): zero for side in range(2) for part in range(2) for g in range(groups)}
    for index, (field, q, z) in enumerate(planes):
        row_index = field * q_count + q
        group, slot = divmod(index, width // 2)
        mine = (lane == 2 * slot) | (lane == 2 * slot + 1)
        for side, shift in ((0, (2 * slot - (width - 2)) % width), (1, (2 * slot) % width)):
            for part, value in enumerate((up_ref[row_index, 2 * z : 2 * z + 2], dn_ref[row_index, 2 * z : 2 * z + 2])):
                key = (side, part, group)
                acc[key] = jnp.where(mine, pltpu.roll(value, shift, 1), acc[key])
    zero_tail = jnp.zeros((ROWS - TOP - height - 2, width), jnp.float32)
    for side, own, out in ((0, own_right_ref, to_right_ref), (1, own_left_ref, to_left_ref)):
        for g in range(groups):
            out[g, 0:TOP] = acc[(side, 0, g)]
            out[g, TOP : TOP + height] = own[g]
            out[g, TOP + height : TOP + height + 2] = acc[(side, 1, g)]
            out[g, TOP + height + 2 : ROWS] = zero_tail


def compute_kernel(f_hbm, cot_hbm, solid_ref, up_hbm, dn_hbm, from_left_ref, from_right_ref,
                   grad_ref, sbar_ref, ef, ec, es, cf, bo, sb2, f_ref, cot_ref, up_ref, dn_ref, sems):
    q_count, layers, height, width = f_ref.shape
    up_copy = pltpu.make_async_copy(up_hbm, up_ref, sems.at[2])
    dn_copy = pltpu.make_async_copy(dn_hbm, dn_ref, sems.at[3])
    f_copy = pltpu.make_async_copy(f_hbm, f_ref, sems.at[0])
    cot_copy = pltpu.make_async_copy(cot_hbm, cot_ref, sems.at[1])
    up_copy.start()
    dn_copy.start()
    f_copy.start()
    cot_copy.start()
    lane = lax.broadcasted_iota(jnp.int32, (ROWS, width), 1)
    low_lanes = lane < 2
    high_lanes = lane >= width - 2
    tail = ROWS - (TOP + height + 2)

    def place_halo(target, index, up_rows, dn_rows):
        group, slot = divmod(index, width // 2)
        from_r = pltpu.roll(from_right_ref[group], (-2 * slot) % width, 1)
        from_l = pltpu.roll(from_left_ref[group], (width - 2 - 2 * slot) % width, 1)
        target[:, width:LANES] = jnp.where(low_lanes, from_r, jnp.where(high_lanes, from_l, 0.0))
        target[TOP + height + 2 : ROWS, 0:width] = jnp.zeros((tail, width), jnp.float32)
        target[TOP - 2 : TOP, 0:width] = up_rows
        target[TOP + height : TOP + height + 2, 0:width] = dn_rows

    targets = []
    up_copy.wait()
    dn_copy.wait()
    for index, (field, q, z) in enumerate(plane_list(q_count, layers)):
        row_index = field * q_count + q
        target = (ef.at[q, z], ec.at[q, z], es.at[z])[field]
        place_halo(target, index, up_ref[row_index, 2 * z : 2 * z + 2], dn_ref[row_index, 2 * z : 2 * z + 2])
        targets.append((field, q, z, target))
    f_copy.wait()
    cot_copy.wait()
    for field, q, z, target in targets:
        if field == 0:
            own = f_ref[q, z]
        elif field == 1:
            own = cot_ref[q, z].astype(jnp.float32)
        else:
            own = solid_ref[z]
        target[TOP : TOP + height, 0:width] = own

    def phase_one(z, carry):
        for k in range((TOP + height + 2 + 7) // 8):
            rows = pl.ds(8 * k, 8)
            out = collide([ef[q, z, rows, :] for q in range(q_count)], es[z, rows, :])
            for q in range(q_count):
                cf[q, z, rows, :] = out[q]
        return carry

    lax.fori_loop(0, layers, phase_one, 0)

    def phase_two(z, carry):
        for k in range((ROWS - 8) // 8):
            start = TOP - 1 + 8 * k
            moved = []
            back = []
            for q in range(q_count):
                ex, ey, ez = int(DIR_X[q]), int(DIR_Y[q]), int(DIR_Z[q])
                src = cf[q, (z - ez + layers) % layers, pl.ds(start - ey, 8), :]
                moved.append(pltpu.roll(src, ex % LANES, 1) if ex else src)
                src = ec[q, (z + ez) % layers, pl.ds(start + ey, 8), :]
                back.append(pltpu.roll(src, (-ex) % LANES, 1) if ex else src)
            ignored, undo = jax.vjp(collide, moved, es[z, pl.ds(start, 8), :])
            grad_field, grad_solid = undo(back)
            for q in range(q_count):
                bo[q, z, pl.ds(8 * k, 8), :] = grad_field[q]
            sb2[z, pl.ds(8 * k, 8), :] = grad_solid
        return carry

    lax.fori_loop(0, layers, phase_two, 0)

    def phase_three(z, carry):
        for k in range(height // 8):
            rows = pl.ds(8 * k, 8)
            pulled = []
            for q in range(q_count):
                ex, ey, ez = int(DIR_X[q]), int(DIR_Y[q]), int(DIR_Z[q])
                src = bo[q, (z + ez) % layers, pl.ds(1 + ey + 8 * k, 8), :]
                if ex:
                    src = pltpu.roll(src, (-ex) % LANES, 1)
                pulled.append(src[:, 0:width])
            field = [f_ref[q, z, rows, :] for q in range(q_count)]
            ignored, undo = jax.vjp(collide, field, solid_ref[z, rows, :])
            grad_field, grad_solid = undo(pulled)
            for q in range(q_count):
                grad_ref[q, z, rows, :] = grad_field[q]
            sbar_ref[z, rows, :] = grad_solid + sb2[z, pl.ds(1 + 8 * k, 8), 0:width]
        return carry

    lax.fori_loop(0, layers, phase_three, 0)


def vmem_specs(count):
    return [pl.BlockSpec(memory_space=pltpu.VMEM) for _ in range(count)]


def on_device(f_start, cotangent, porosity, brick_ids, brick_slot):
    q_count, layers_dev, rows_dev, cols_dev = f_start.shape
    nx = lax.axis_size("gx")
    ny = lax.axis_size("gy")
    tile_count = cols_dev // 128
    brick_count = layers_dev * rows_dev * tile_count
    listed = brick_ids.reshape(-1)
    slots_of = brick_slot.reshape(-1)
    slot_table = porosity.reshape(-1)
    brick_hit = (listed[:, None] == jnp.arange(brick_count, dtype=jnp.int32)[None, :]).astype(
        jnp.float32
    )
    slot_hit = (
        slots_of[:, None] == jnp.arange(slot_table.shape[0], dtype=jnp.int32)[None, :]
    ).astype(jnp.float32)
    brick_value = jnp.sum(slot_hit * slot_table[None, :], axis=1)
    tile_value = jnp.sum(brick_hit * brick_value[:, None], axis=0)
    solid = jnp.broadcast_to(
        tile_value.reshape(layers_dev, rows_dev, tile_count, 1),
        (layers_dev, rows_dev, tile_count, 128),
    ).reshape(layers_dev, rows_dev, cols_dev)

    def shift(value, axis, size, step):
        return lax.ppermute(value, axis, [(i, (i + step) % size) for i in range(size)])

    cot32 = cotangent.astype(jnp.float32)
    def edge_rows(chosen):
        rows = jnp.concatenate([f_start[:, :, chosen], cot32[:, :, chosen], solid[None, :, chosen]], axis=0)
        return rows.reshape(rows.shape[0], 2 * layers_dev, cols_dev)

    first_rows = edge_rows(slice(0, 2))
    last_rows = edge_rows(slice(rows_dev - 2, rows_dev))
    up_rows = shift(last_rows, "gy", ny, 1)
    dn_rows = shift(first_rows, "gy", ny, -1)
    plane_count = (2 * q_count + 1) * layers_dev
    groups = -(-plane_count // (cols_dev // 2))
    buffer = jax.ShapeDtypeStruct((groups, ROWS, cols_dev), jnp.float32)
    own_buffer = jax.ShapeDtypeStruct((groups, rows_dev, cols_dev), jnp.float32)
    own_right, own_left = pl.pallas_call(
        pack_own_kernel,
        out_shape=(own_buffer, own_buffer),
        in_specs=vmem_specs(3),
        out_specs=tuple(vmem_specs(2)),
    )(f_start, cotangent, solid)
    to_right, to_left = pl.pallas_call(
        pack_edge_kernel,
        out_shape=(buffer, buffer),
        in_specs=vmem_specs(2) + [pl.BlockSpec(memory_space=pltpu.HBM)] * 2,
        out_specs=tuple(vmem_specs(2)),
        scratch_shapes=[
            pltpu.VMEM(up_rows.shape, jnp.float32),
            pltpu.VMEM(dn_rows.shape, jnp.float32),
            pltpu.SemaphoreType.DMA((2,)),
        ],
    )(own_right, own_left, up_rows, dn_rows)
    from_left = shift(to_right, "gx", nx, 1)
    from_right = shift(to_left, "gx", nx, -1)
    big = pltpu.VMEM((q_count, layers_dev, ROWS, LANES), jnp.float32)
    start_grad, solid_bar = pl.pallas_call(
        compute_kernel,
        out_shape=(
            jax.ShapeDtypeStruct(f_start.shape, jnp.float32),
            jax.ShapeDtypeStruct(solid.shape, jnp.float32),
        ),
        in_specs=[pl.BlockSpec(memory_space=pltpu.HBM)] * 2 + vmem_specs(1)
        + [pl.BlockSpec(memory_space=pltpu.HBM)] * 2 + vmem_specs(2),
        out_specs=tuple(vmem_specs(2)),
        scratch_shapes=[
            big,
            big,
            pltpu.VMEM((layers_dev, ROWS, LANES), jnp.float32),
            big,
            pltpu.VMEM((q_count, layers_dev, ROWS - 8, LANES), jnp.float32),
            pltpu.VMEM((layers_dev, ROWS - 8, LANES), jnp.float32),
            pltpu.VMEM(f_start.shape, jnp.float32),
            pltpu.VMEM(cotangent.shape, cotangent.dtype),
            pltpu.VMEM(up_rows.shape, jnp.float32),
            pltpu.VMEM(dn_rows.shape, jnp.float32),
            pltpu.SemaphoreType.DMA((4,)),
        ],
        compiler_params=pltpu.CompilerParams(vmem_limit_bytes=28 * 1024 * 1024),
    )(f_start, cotangent, solid, up_rows, dn_rows, from_left, from_right)
    tile_sums = jnp.sum(solid_bar.reshape(brick_count, 128), axis=1)
    brick_sum = jnp.sum(brick_hit * tile_sums[None, :], axis=1)
    slot_grad = jnp.sum(slot_hit * brick_sum[:, None], axis=0)
    return (start_grad, slot_grad.reshape(porosity.shape))


def solution(mesh):
    return jax.shard_map(
        on_device,
        mesh=mesh,
        in_specs=(
            P(None, None, "gy", "gx"),
            P(None, None, "gy", "gx"),
            P("gx", "gy", None),
            P("gx", "gy", None),
            P("gx", "gy", None),
        ),
        out_specs=(P(None, None, "gy", "gx"), P("gx", "gy", None)),
        check_vma=False,
    )
```

```python
import jax
import jax.numpy as jnp
import numpy as np
from jax import lax
from jax.experimental import pallas as pl
from jax.experimental.pallas import tpu as pltpu
from jax.sharding import PartitionSpec as P

DIR_X = np.array([0, 1, -1, 0, 0, 0, 0, 1, -1, 1, -1, 1, -1, 1, -1, 0, 0, 0, 0])
DIR_Y = np.array([0, 0, 0, 1, -1, 0, 0, 1, 1, -1, -1, 0, 0, 0, 0, 1, -1, 1, -1])
DIR_Z = np.array([0, 0, 0, 0, 0, 1, -1, 0, 0, 0, 0, 1, 1, -1, -1, 1, 1, -1, -1])
WEIGHTS = np.array([1.0 / 3.0] + [1.0 / 18.0] * 6 + [1.0 / 36.0] * 12)
RELAX_RATE = 0.8

ROWS = 48
LANES = 256
TOP = 2


def collide(fields, solid):
    density = fields[0]
    for value in fields[1:]:
        density = density + value
    inverse = (1.0 - solid) / density
    moments = []
    for direction in (DIR_X, DIR_Y, DIR_Z):
        total = None
        for q in range(19):
            if direction[q] == 0:
                continue
            term = fields[q] if direction[q] > 0 else -fields[q]
            total = term if total is None else total + term
        moments.append(total * inverse)
    vel_x, vel_y, vel_z = moments
    square = vel_x * vel_x + vel_y * vel_y + vel_z * vel_z
    out = []
    for q in range(19):
        along = None
        for sign, vel in ((DIR_X[q], vel_x), (DIR_Y[q], vel_y), (DIR_Z[q], vel_z)):
            if sign == 0:
                continue
            term = vel if sign > 0 else -vel
            along = term if along is None else along + term
        if along is None:
            shape = 1.0 - 1.5 * square
        else:
            shape = 1.0 + 3.0 * along + 4.5 * along * along - 1.5 * square
        balance = float(WEIGHTS[q]) * density * shape
        out.append(fields[q] - RELAX_RATE * (fields[q] - balance))
    return out


def collide_vjp(fields, solid, cots):
    density = fields[0]
    for value in fields[1:]:
        density = density + value
    recip = 1.0 / density
    scale = (1.0 - solid) * recip
    moments = []
    for direction in (DIR_X, DIR_Y, DIR_Z):
        total = None
        for q in range(19):
            if direction[q] == 0:
                continue
            term = fields[q] if direction[q] > 0 else -fields[q]
            total = term if total is None else total + term
        moments.append(total)
    vel = [m * scale for m in moments]
    square = vel[0] * vel[0] + vel[1] * vel[1] + vel[2] * vel[2]
    weighted_sum = None
    density_part = None
    dv = [None, None, None]
    for q in range(19):
        weighted = (RELAX_RATE * float(WEIGHTS[q])) * cots[q]
        weighted_sum = weighted if weighted_sum is None else weighted_sum + weighted
        along = None
        for sign, v in zip((DIR_X[q], DIR_Y[q], DIR_Z[q]), vel):
            if sign == 0:
                continue
            term = v if sign > 0 else -v
            along = term if along is None else along + term
        if along is None:
            shape = 1.0 - 1.5 * square
        else:
            shape = 1.0 + along * (3.0 + 4.5 * along) - 1.5 * square
            slope = weighted * (3.0 + 9.0 * along)
            for axis, sign in enumerate((DIR_X[q], DIR_Y[q], DIR_Z[q])):
                if sign == 0:
                    continue
                term = slope if sign > 0 else -slope
                dv[axis] = term if dv[axis] is None else dv[axis] + term
        part = weighted * shape
        density_part = part if density_part is None else density_part + part
    dv = [density * (d - 3.0 * v * weighted_sum) for d, v in zip(dv, vel)]
    through = (moments[0] * dv[0] + moments[1] * dv[1] + moments[2] * dv[2]) * recip
    common = density_part - scale * through
    scaled = [scale * d for d in dv]
    grads = []
    for q in range(19):
        grad = (1.0 - RELAX_RATE) * cots[q] + common
        for sign, d in zip((DIR_X[q], DIR_Y[q], DIR_Z[q]), scaled):
            if sign == 0:
                continue
            grad = grad + d if sign > 0 else grad - d
        grads.append(grad)
    return grads, -through


def plane_list(q_count, layers):
    planes = [(0, q, z) for q in range(q_count) for z in range(layers)]
    planes += [(1, q, z) for q in range(q_count) for z in range(layers)]
    planes += [(2, 0, z) for z in range(layers)]
    return planes


def pack_own_kernel(f_ref, cot_ref, solid_ref, to_right_ref, to_left_ref):
    q_count, layers, height, width = f_ref.shape
    groups = to_right_ref.shape[0]
    lane = lax.broadcasted_iota(jnp.int32, (height, width), 1)
    zero = jnp.zeros((height, width), jnp.float32)
    acc = {(side, g): zero for side in range(2) for g in range(groups)}
    for index, (field, q, z) in enumerate(plane_list(q_count, layers)):
        if field == 0:
            own = f_ref[q, z]
        elif field == 1:
            own = cot_ref[q, z].astype(jnp.float32)
        else:
            own = solid_ref[z]
        group, slot = divmod(index, width // 2)
        mine = (lane == 2 * slot) | (lane == 2 * slot + 1)
        for side, shift in ((0, (2 * slot - (width - 2)) % width), (1, (2 * slot) % width)):
            acc[(side, group)] = jnp.where(mine, pltpu.roll(own, shift, 1), acc[(side, group)])
    for side, out in ((0, to_right_ref), (1, to_left_ref)):
        for g in range(groups):
            out[g] = acc[(side, g)]


def pack_edge_kernel(own_right_ref, own_left_ref, up_ref, dn_ref, to_right_ref, to_left_ref):
    groups, height, width = own_right_ref.shape
    planes = plane_list((up_ref.shape[0] - 1) // 2, up_ref.shape[1])
    q_count = (up_ref.shape[0] - 1) // 2
    lane = lax.broadcasted_iota(jnp.int32, (2, width), 1)
    zero = jnp.zeros((2, width), jnp.float32)
    acc = {(side, part, g): zero for side in range(2) for part in range(2) for g in range(groups)}
    for index, (field, q, z) in enumerate(planes):
        row_index = field * q_count + q
        group, slot = divmod(index, width // 2)
        mine = (lane == 2 * slot) | (lane == 2 * slot + 1)
        for side, shift in ((0, (2 * slot - (width - 2)) % width), (1, (2 * slot) % width)):
            for part, value in enumerate((up_ref[row_index, z], dn_ref[row_index, z])):
                key = (side, part, group)
                acc[key] = jnp.where(mine, pltpu.roll(value, shift, 1), acc[key])
    zero_tail = jnp.zeros((ROWS - TOP - height - 2, width), jnp.float32)
    for side, own, out in ((0, own_right_ref, to_right_ref), (1, own_left_ref, to_left_ref)):
        for g in range(groups):
            out[g, 0:TOP] = acc[(side, 0, g)]
            out[g, TOP : TOP + height] = own[g]
            out[g, TOP + height : TOP + height + 2] = acc[(side, 1, g)]
            out[g, TOP + height + 2 : ROWS] = zero_tail


def compute_kernel(f_hbm, cot_hbm, solid_ref, up_ref, dn_ref, from_left_ref, from_right_ref,
                   grad_ref, sbar_ref, ef, ec, es, cf, bo, sb2, f_ref, cot_ref, sems):
    q_count, layers, height, width = f_ref.shape
    f_copy = pltpu.make_async_copy(f_hbm, f_ref, sems.at[0])
    cot_copy = pltpu.make_async_copy(cot_hbm, cot_ref, sems.at[1])
    f_copy.start()
    cot_copy.start()
    lane = lax.broadcasted_iota(jnp.int32, (ROWS, width), 1)
    low_lanes = lane < 2
    high_lanes = lane >= width - 2
    tail = ROWS - (TOP + height + 2)

    def place_halo(target, index, up_rows, dn_rows):
        group, slot = divmod(index, width // 2)
        from_r = pltpu.roll(from_right_ref[group], (-2 * slot) % width, 1)
        from_l = pltpu.roll(from_left_ref[group], (width - 2 - 2 * slot) % width, 1)
        target[:, width:LANES] = jnp.where(low_lanes, from_r, jnp.where(high_lanes, from_l, 0.0))
        target[TOP + height + 2 : ROWS, 0:width] = jnp.zeros((tail, width), jnp.float32)
        target[TOP - 2 : TOP, 0:width] = up_rows
        target[TOP + height : TOP + height + 2, 0:width] = dn_rows

    targets = []
    for index, (field, q, z) in enumerate(plane_list(q_count, layers)):
        row_index = field * q_count + q
        target = (ef.at[q, z], ec.at[q, z], es.at[z])[field]
        place_halo(target, index, up_ref[row_index, z], dn_ref[row_index, z])
        targets.append((field, q, z, target))
    f_copy.wait()
    cot_copy.wait()
    for field, q, z, target in targets:
        if field == 0:
            own = f_ref[q, z]
        elif field == 1:
            own = cot_ref[q, z].astype(jnp.float32)
        else:
            own = solid_ref[z]
        target[TOP : TOP + height, 0:width] = own

    def phase_one(z, carry):
        for k in range((TOP + height + 2 + 7) // 8):
            rows = pl.ds(8 * k, 8)
            out = collide([ef[q, z, rows, :] for q in range(q_count)], es[z, rows, :])
            for q in range(q_count):
                cf[q, z, rows, :] = out[q]
        return carry

    lax.fori_loop(0, layers, phase_one, 0)

    def phase_two(z, carry):
        for k in range((ROWS - 8) // 8):
            start = TOP - 1 + 8 * k
            moved = []
            back = []
            for q in range(q_count):
                ex, ey, ez = int(DIR_X[q]), int(DIR_Y[q]), int(DIR_Z[q])
                src = cf[q, (z - ez + layers) % layers, pl.ds(start - ey, 8), :]
                moved.append(pltpu.roll(src, ex % LANES, 1) if ex else src)
                src = ec[q, (z + ez) % layers, pl.ds(start + ey, 8), :]
                back.append(pltpu.roll(src, (-ex) % LANES, 1) if ex else src)
            grad_field, grad_solid = collide_vjp(moved, es[z, pl.ds(start, 8), :], back)
            for q in range(q_count):
                bo[q, z, pl.ds(8 * k, 8), :] = grad_field[q]
            sb2[z, pl.ds(8 * k, 8), :] = grad_solid
        return carry

    lax.fori_loop(0, layers, phase_two, 0)

    def phase_three(z, carry):
        for k in range(height // 8):
            rows = pl.ds(8 * k, 8)
            pulled = []
            for q in range(q_count):
                ex, ey, ez = int(DIR_X[q]), int(DIR_Y[q]), int(DIR_Z[q])
                src = bo[q, (z + ez) % layers, pl.ds(1 + ey + 8 * k, 8), :]
                if ex:
                    src = pltpu.roll(src, (-ex) % LANES, 1)
                pulled.append(src[:, 0:width])
            field = [f_ref[q, z, rows, :] for q in range(q_count)]
            grad_field, grad_solid = collide_vjp(field, solid_ref[z, rows, :], pulled)
            for q in range(q_count):
                grad_ref[q, z, rows, :] = grad_field[q]
            sbar_ref[z, rows, :] = grad_solid + sb2[z, pl.ds(1 + 8 * k, 8), 0:width]
        return carry

    lax.fori_loop(0, layers, phase_three, 0)


def vmem_specs(count):
    return [pl.BlockSpec(memory_space=pltpu.VMEM) for _ in range(count)]


def on_device(f_start, cotangent, porosity, brick_ids, brick_slot):
    q_count, layers_dev, rows_dev, cols_dev = f_start.shape
    nx = lax.axis_size("gx")
    ny = lax.axis_size("gy")
    tile_count = cols_dev // 128
    brick_count = layers_dev * rows_dev * tile_count
    listed = brick_ids.reshape(-1)
    slots_of = brick_slot.reshape(-1)
    slot_table = porosity.reshape(-1)
    brick_hit = (listed[:, None] == jnp.arange(brick_count, dtype=jnp.int32)[None, :]).astype(
        jnp.float32
    )
    slot_hit = (
        slots_of[:, None] == jnp.arange(slot_table.shape[0], dtype=jnp.int32)[None, :]
    ).astype(jnp.float32)
    brick_value = jnp.sum(slot_hit * slot_table[None, :], axis=1)
    tile_value = jnp.sum(brick_hit * brick_value[:, None], axis=0)
    solid = jnp.broadcast_to(
        tile_value.reshape(layers_dev, rows_dev, tile_count, 1),
        (layers_dev, rows_dev, tile_count, 128),
    ).reshape(layers_dev, rows_dev, cols_dev)

    def shift(value, axis, size, step):
        return lax.ppermute(value, axis, [(i, (i + step) % size) for i in range(size)])

    cot32 = cotangent.astype(jnp.float32)
    first_rows = jnp.concatenate([f_start[:, :, 0:2], cot32[:, :, 0:2], solid[None, :, 0:2]], axis=0)
    last_rows = jnp.concatenate(
        [f_start[:, :, rows_dev - 2 :], cot32[:, :, rows_dev - 2 :], solid[None, :, rows_dev - 2 :]],
        axis=0,
    )
    up_rows = shift(last_rows, "gy", ny, 1)
    dn_rows = shift(first_rows, "gy", ny, -1)
    plane_count = (2 * q_count + 1) * layers_dev
    groups = -(-plane_count // (cols_dev // 2))
    buffer = jax.ShapeDtypeStruct((groups, ROWS, cols_dev), jnp.float32)
    own_buffer = jax.ShapeDtypeStruct((groups, rows_dev, cols_dev), jnp.float32)
    own_right, own_left = pl.pallas_call(
        pack_own_kernel,
        out_shape=(own_buffer, own_buffer),
        in_specs=vmem_specs(3),
        out_specs=tuple(vmem_specs(2)),
    )(f_start, cotangent, solid)
    to_right, to_left = pl.pallas_call(
        pack_edge_kernel,
        out_shape=(buffer, buffer),
        in_specs=vmem_specs(4),
        out_specs=tuple(vmem_specs(2)),
    )(own_right, own_left, up_rows, dn_rows)
    from_left = shift(to_right, "gx", nx, 1)
    from_right = shift(to_left, "gx", nx, -1)
    big = pltpu.VMEM((q_count, layers_dev, ROWS, LANES), jnp.float32)
    start_grad, solid_bar = pl.pallas_call(
        compute_kernel,
        out_shape=(
            jax.ShapeDtypeStruct(f_start.shape, jnp.float32),
            jax.ShapeDtypeStruct(solid.shape, jnp.float32),
        ),
        in_specs=[pl.BlockSpec(memory_space=pl.ANY)] * 2 + vmem_specs(5),
        out_specs=tuple(vmem_specs(2)),
        scratch_shapes=[
            big,
            big,
            pltpu.VMEM((layers_dev, ROWS, LANES), jnp.float32),
            big,
            pltpu.VMEM((q_count, layers_dev, ROWS - 8, LANES), jnp.float32),
            pltpu.VMEM((layers_dev, ROWS - 8, LANES), jnp.float32),
            pltpu.VMEM(f_start.shape, jnp.float32),
            pltpu.VMEM(cotangent.shape, cotangent.dtype),
            pltpu.SemaphoreType.DMA((2,)),
        ],
        compiler_params=pltpu.CompilerParams(vmem_limit_bytes=48 * 1024 * 1024),
    )(f_start, cotangent, solid, up_rows, dn_rows, from_left, from_right)
    tile_sums = jnp.sum(solid_bar.reshape(brick_count, 128), axis=1)
    brick_sum = jnp.sum(brick_hit * tile_sums[None, :], axis=1)
    slot_grad = jnp.sum(slot_hit * brick_sum[:, None], axis=0)
    return (start_grad, slot_grad.reshape(porosity.shape))


def solution(mesh):
    return jax.shard_map(
        on_device,
        mesh=mesh,
        in_specs=(
            P(None, None, "gy", "gx"),
            P(None, None, "gy", "gx"),
            P("gx", "gy", None),
            P("gx", "gy", None),
            P("gx", "gy", None),
        ),
        out_specs=(P(None, None, "gy", "gx"), P("gx", "gy", None)),
        check_vma=False,
    )
```

```python
import jax
import jax.numpy as jnp
import numpy as np
from jax import lax
from jax.experimental import pallas as pl
from jax.experimental.pallas import tpu as pltpu
from jax.sharding import PartitionSpec as P

DIR_X = np.array([0, 1, -1, 0, 0, 0, 0, 1, -1, 1, -1, 1, -1, 1, -1, 0, 0, 0, 0])
DIR_Y = np.array([0, 0, 0, 1, -1, 0, 0, 1, 1, -1, -1, 0, 0, 0, 0, 1, -1, 1, -1])
DIR_Z = np.array([0, 0, 0, 0, 0, 1, -1, 0, 0, 0, 0, 1, 1, -1, -1, 1, 1, -1, -1])
WEIGHTS = np.array([1.0 / 3.0] + [1.0 / 18.0] * 6 + [1.0 / 36.0] * 12)
RELAX_RATE = 0.8

ROWS = 48
LANES = 256
TOP = 2


def collide(fields, solid):
    density = fields[0]
    for value in fields[1:]:
        density = density + value
    inverse = (1.0 - solid) / density
    moments = []
    for direction in (DIR_X, DIR_Y, DIR_Z):
        total = None
        for q in range(19):
            if direction[q] == 0:
                continue
            term = fields[q] if direction[q] > 0 else -fields[q]
            total = term if total is None else total + term
        moments.append(total * inverse)
    vel_x, vel_y, vel_z = moments
    square = vel_x * vel_x + vel_y * vel_y + vel_z * vel_z
    out = []
    for q in range(19):
        along = None
        for sign, vel in ((DIR_X[q], vel_x), (DIR_Y[q], vel_y), (DIR_Z[q], vel_z)):
            if sign == 0:
                continue
            term = vel if sign > 0 else -vel
            along = term if along is None else along + term
        if along is None:
            shape = 1.0 - 1.5 * square
        else:
            shape = 1.0 + 3.0 * along + 4.5 * along * along - 1.5 * square
        balance = float(WEIGHTS[q]) * density * shape
        out.append(fields[q] - RELAX_RATE * (fields[q] - balance))
    return out


def collide_vjp(fields, solid, cots):
    density = fields[0]
    for value in fields[1:]:
        density = density + value
    recip = 1.0 / density
    scale = (1.0 - solid) * recip
    moments = []
    for direction in (DIR_X, DIR_Y, DIR_Z):
        total = None
        for q in range(19):
            if direction[q] == 0:
                continue
            term = fields[q] if direction[q] > 0 else -fields[q]
            total = term if total is None else total + term
        moments.append(total)
    vel = [m * scale for m in moments]
    square = vel[0] * vel[0] + vel[1] * vel[1] + vel[2] * vel[2]
    weighted_sum = None
    density_part = None
    dv = [None, None, None]
    for q in range(19):
        weighted = (RELAX_RATE * float(WEIGHTS[q])) * cots[q]
        weighted_sum = weighted if weighted_sum is None else weighted_sum + weighted
        along = None
        for sign, v in zip((DIR_X[q], DIR_Y[q], DIR_Z[q]), vel):
            if sign == 0:
                continue
            term = v if sign > 0 else -v
            along = term if along is None else along + term
        if along is None:
            shape = 1.0 - 1.5 * square
        else:
            shape = 1.0 + along * (3.0 + 4.5 * along) - 1.5 * square
            slope = weighted * (3.0 + 9.0 * along)
            for axis, sign in enumerate((DIR_X[q], DIR_Y[q], DIR_Z[q])):
                if sign == 0:
                    continue
                term = slope if sign > 0 else -slope
                dv[axis] = term if dv[axis] is None else dv[axis] + term
        part = weighted * shape
        density_part = part if density_part is None else density_part + part
    dv = [density * (d - 3.0 * v * weighted_sum) for d, v in zip(dv, vel)]
    through = (moments[0] * dv[0] + moments[1] * dv[1] + moments[2] * dv[2]) * recip
    common = density_part - scale * through
    scaled = [scale * d for d in dv]
    grads = []
    for q in range(19):
        grad = (1.0 - RELAX_RATE) * cots[q] + common
        for sign, d in zip((DIR_X[q], DIR_Y[q], DIR_Z[q]), scaled):
            if sign == 0:
                continue
            grad = grad + d if sign > 0 else grad - d
        grads.append(grad)
    return grads, -through


def plane_list(q_count, layers):
    planes = [(0, q, z) for q in range(q_count) for z in range(layers)]
    planes += [(1, q, z) for q in range(q_count) for z in range(layers)]
    planes += [(2, 0, z) for z in range(layers)]
    return planes


def pack_kernel(f_ref, cot_ref, solid_ref, packed_ref):
    q_count, layers, height, width = f_ref.shape
    groups = packed_ref.shape[0]
    lane = lax.broadcasted_iota(jnp.int32, (height, width), 1)
    zero = jnp.zeros((height, width), jnp.float32)
    acc = [zero for g in range(groups)]
    for index, (field, q, z) in enumerate(plane_list(q_count, layers)):
        if field == 0:
            own = f_ref[q, z]
        elif field == 1:
            own = cot_ref[q, z].astype(jnp.float32)
        else:
            own = solid_ref[z]
        group, slot = divmod(index, width // 4)
        mine = (lane >= 4 * slot) & (lane < 4 * slot + 4)
        acc[group] = jnp.where(mine, pltpu.roll(own, (4 * slot - (width - 2)) % width, 1), acc[group])
    for g in range(groups):
        packed_ref[g] = acc[g]


def compute_kernel(f_hbm, cot_hbm, solid_ref, up_ref, dn_ref, from_left_ref, from_right_ref,
                   grad_ref, sbar_ref, ef, ec, es, cf, bo, sb2, f_ref, cot_ref, sems):
    q_count, layers, height, width = f_ref.shape
    groups = from_left_ref.shape[0]
    corner_base = (2 * q_count + 1) * layers * 2
    f_copy = pltpu.make_async_copy(f_hbm, f_ref, sems.at[0])
    cot_copy = pltpu.make_async_copy(cot_hbm, cot_ref, sems.at[1])
    f_copy.start()
    cot_copy.start()
    lane_own = lax.broadcasted_iota(jnp.int32, (height, width), 1)
    lane_edge = lax.broadcasted_iota(jnp.int32, (2, width), 1)
    tail = ROWS - (TOP + height + 2)

    def sides(left, right, slot, lane):
        from_r = pltpu.roll(right, (-(4 * slot + 2)) % width, 1)
        from_l = pltpu.roll(left, (width - 2 - 4 * slot) % width, 1)
        return jnp.where(lane < 2, from_r, jnp.where(lane >= width - 2, from_l, 0.0))

    def place_halo(target, index, row_index, z):
        group, slot = divmod(index, width // 4)
        base = (row_index * layers + z) * 2
        left_rows = corner_base + 2 * group
        right_rows = corner_base + 2 * (groups + group)
        target[TOP : TOP + height, width:LANES] = sides(
            from_left_ref[group], from_right_ref[group], slot, lane_own)
        target[0:TOP, width:LANES] = sides(
            up_ref[left_rows : left_rows + 2], up_ref[right_rows : right_rows + 2], slot, lane_edge)
        target[TOP + height : TOP + height + 2, width:LANES] = sides(
            dn_ref[left_rows : left_rows + 2], dn_ref[right_rows : right_rows + 2], slot, lane_edge)
        target[TOP + height + 2 : ROWS, :] = jnp.zeros((tail, LANES), jnp.float32)
        target[0:TOP, 0:width] = up_ref[base : base + 2]
        target[TOP + height : TOP + height + 2, 0:width] = dn_ref[base : base + 2]

    targets = []
    for index, (field, q, z) in enumerate(plane_list(q_count, layers)):
        row_index = field * q_count + q
        target = (ef.at[q, z], ec.at[q, z], es.at[z])[field]
        place_halo(target, index, row_index, z)
        targets.append((field, q, z, target))
    f_copy.wait()
    cot_copy.wait()
    for field, q, z, target in targets:
        if field == 0:
            own = f_ref[q, z]
        elif field == 1:
            own = cot_ref[q, z].astype(jnp.float32)
        else:
            own = solid_ref[z]
        target[TOP : TOP + height, 0:width] = own

    def phase_one(z, carry):
        for k in range((TOP + height + 2 + 7) // 8):
            rows = pl.ds(8 * k, 8)
            out = collide([ef[q, z, rows, :] for q in range(q_count)], es[z, rows, :])
            for q in range(q_count):
                cf[q, z, rows, :] = out[q]
        return carry

    lax.fori_loop(0, layers, phase_one, 0)

    def phase_two(z, carry):
        for k in range((ROWS - 8) // 8):
            start = TOP - 1 + 8 * k
            moved = []
            back = []
            for q in range(q_count):
                ex, ey, ez = int(DIR_X[q]), int(DIR_Y[q]), int(DIR_Z[q])
                src = cf[q, (z - ez + layers) % layers, pl.ds(start - ey, 8), :]
                moved.append(pltpu.roll(src, ex % LANES, 1) if ex else src)
                src = ec[q, (z + ez) % layers, pl.ds(start + ey, 8), :]
                back.append(pltpu.roll(src, (-ex) % LANES, 1) if ex else src)
            grad_field, grad_solid = collide_vjp(moved, es[z, pl.ds(start, 8), :], back)
            for q in range(q_count):
                bo[q, z, pl.ds(8 * k, 8), :] = grad_field[q]
            sb2[z, pl.ds(8 * k, 8), :] = grad_solid
        return carry

    lax.fori_loop(0, layers, phase_two, 0)

    def phase_three(z, carry):
        for k in range(height // 8):
            rows = pl.ds(8 * k, 8)
            pulled = []
            for q in range(q_count):
                ex, ey, ez = int(DIR_X[q]), int(DIR_Y[q]), int(DIR_Z[q])
                src = bo[q, (z + ez) % layers, pl.ds(1 + ey + 8 * k, 8), :]
                if ex:
                    src = pltpu.roll(src, (-ex) % LANES, 1)
                pulled.append(src[:, 0:width])
            field = [f_ref[q, z, rows, :] for q in range(q_count)]
            grad_field, grad_solid = collide_vjp(field, solid_ref[z, rows, :], pulled)
            for q in range(q_count):
                grad_ref[q, z, rows, :] = grad_field[q]
            sbar_ref[z, rows, :] = grad_solid + sb2[z, pl.ds(1 + 8 * k, 8), 0:width]
        return carry

    lax.fori_loop(0, layers, phase_three, 0)


def vmem_specs(count):
    return [pl.BlockSpec(memory_space=pltpu.VMEM) for _ in range(count)]


def on_device(f_start, cotangent, porosity, brick_ids, brick_slot):
    q_count, layers_dev, rows_dev, cols_dev = f_start.shape
    nx = lax.axis_size("gx")
    ny = lax.axis_size("gy")
    tile_count = cols_dev // 128
    brick_count = layers_dev * rows_dev * tile_count
    listed = brick_ids.reshape(-1)
    slots_of = brick_slot.reshape(-1)
    slot_table = porosity.reshape(-1)
    brick_hit = (listed[:, None] == jnp.arange(brick_count, dtype=jnp.int32)[None, :]).astype(
        jnp.float32
    )
    slot_hit = (
        slots_of[:, None] == jnp.arange(slot_table.shape[0], dtype=jnp.int32)[None, :]
    ).astype(jnp.float32)
    brick_value = jnp.sum(slot_hit * slot_table[None, :], axis=1)
    tile_value = jnp.sum(brick_hit * brick_value[:, None], axis=0)
    solid = jnp.broadcast_to(
        tile_value.reshape(layers_dev, rows_dev, tile_count, 1),
        (layers_dev, rows_dev, tile_count, 128),
    ).reshape(layers_dev, rows_dev, cols_dev)

    def shift(value, axis, size, step):
        return lax.ppermute(value, axis, [(i, (i + step) % size) for i in range(size)])

    cot32 = cotangent.astype(jnp.float32)
    plane_count = (2 * q_count + 1) * layers_dev
    groups = -(-plane_count // (cols_dev // 4))
    packed = pl.pallas_call(
        pack_kernel,
        out_shape=jax.ShapeDtypeStruct((groups, rows_dev, cols_dev), jnp.float32),
        in_specs=vmem_specs(3),
        out_specs=vmem_specs(1)[0],
    )(f_start, cotangent, solid)
    from_left = shift(packed, "gx", nx, 1)
    from_right = shift(packed, "gx", nx, -1)

    def edge_rows(chosen):
        rows = jnp.concatenate([f_start[:, :, chosen], cot32[:, :, chosen], solid[None, :, chosen]], axis=0)
        corners = jnp.concatenate([from_left[:, chosen], from_right[:, chosen]], axis=0)
        return jnp.concatenate(
            [rows.reshape(-1, cols_dev), corners.reshape(-1, cols_dev)], axis=0
        )

    first_rows = edge_rows(slice(0, 2))
    last_rows = edge_rows(slice(rows_dev - 2, rows_dev))
    up_rows = shift(last_rows, "gy", ny, 1)
    dn_rows = shift(first_rows, "gy", ny, -1)
    big = pltpu.VMEM((q_count, layers_dev, ROWS, LANES), jnp.float32)
    start_grad, solid_bar = pl.pallas_call(
        compute_kernel,
        out_shape=(
            jax.ShapeDtypeStruct(f_start.shape, jnp.float32),
            jax.ShapeDtypeStruct(solid.shape, jnp.float32),
        ),
        in_specs=[pl.BlockSpec(memory_space=pl.ANY)] * 2 + vmem_specs(5),
        out_specs=tuple(vmem_specs(2)),
        scratch_shapes=[
            big,
            big,
            pltpu.VMEM((layers_dev, ROWS, LANES), jnp.float32),
            big,
            pltpu.VMEM((q_count, layers_dev, ROWS - 8, LANES), jnp.float32),
            pltpu.VMEM((layers_dev, ROWS - 8, LANES), jnp.float32),
            pltpu.VMEM(f_start.shape, jnp.float32),
            pltpu.VMEM(cotangent.shape, cotangent.dtype),
            pltpu.SemaphoreType.DMA((2,)),
        ],
        compiler_params=pltpu.CompilerParams(vmem_limit_bytes=48 * 1024 * 1024),
    )(f_start, cotangent, solid, up_rows, dn_rows, from_left, from_right)
    tile_sums = jnp.sum(solid_bar.reshape(brick_count, 128), axis=1)
    brick_sum = jnp.sum(brick_hit * tile_sums[None, :], axis=1)
    slot_grad = jnp.sum(slot_hit * brick_sum[:, None], axis=0)
    return (start_grad, slot_grad.reshape(porosity.shape))


def solution(mesh):
    return jax.shard_map(
        on_device,
        mesh=mesh,
        in_specs=(
            P(None, None, "gy", "gx"),
            P(None, None, "gy", "gx"),
            P("gx", "gy", None),
            P("gx", "gy", None),
            P("gx", "gy", None),
        ),
        out_specs=(P(None, None, "gy", "gx"), P("gx", "gy", None)),
        check_vma=False,
    )
```

```python
import jax
import jax.numpy as jnp
import numpy as np
from jax import lax
from jax.experimental import pallas as pl
from jax.experimental.pallas import tpu as pltpu
from jax.sharding import PartitionSpec as P

DIR_X = np.array([0, 1, -1, 0, 0, 0, 0, 1, -1, 1, -1, 1, -1, 1, -1, 0, 0, 0, 0])
DIR_Y = np.array([0, 0, 0, 1, -1, 0, 0, 1, 1, -1, -1, 0, 0, 0, 0, 1, -1, 1, -1])
DIR_Z = np.array([0, 0, 0, 0, 0, 1, -1, 0, 0, 0, 0, 1, 1, -1, -1, 1, 1, -1, -1])
WEIGHTS = np.array([1.0 / 3.0] + [1.0 / 18.0] * 6 + [1.0 / 36.0] * 12)
RELAX_RATE = 0.8

ROWS = 48
LANES = 256
TOP = 2


def collide(fields, solid):
    density = fields[0]
    for value in fields[1:]:
        density = density + value
    inverse = (1.0 - solid) / density
    moments = []
    for direction in (DIR_X, DIR_Y, DIR_Z):
        total = None
        for q in range(19):
            if direction[q] == 0:
                continue
            term = fields[q] if direction[q] > 0 else -fields[q]
            total = term if total is None else total + term
        moments.append(total * inverse)
    vel_x, vel_y, vel_z = moments
    square = vel_x * vel_x + vel_y * vel_y + vel_z * vel_z
    out = []
    for q in range(19):
        along = None
        for sign, vel in ((DIR_X[q], vel_x), (DIR_Y[q], vel_y), (DIR_Z[q], vel_z)):
            if sign == 0:
                continue
            term = vel if sign > 0 else -vel
            along = term if along is None else along + term
        if along is None:
            shape = 1.0 - 1.5 * square
        else:
            shape = 1.0 + 3.0 * along + 4.5 * along * along - 1.5 * square
        balance = float(WEIGHTS[q]) * density * shape
        out.append(fields[q] - RELAX_RATE * (fields[q] - balance))
    return out


def collide_vjp(fields, solid, cots):
    density = fields[0]
    for value in fields[1:]:
        density = density + value
    recip = 1.0 / density
    scale = (1.0 - solid) * recip
    moments = []
    for direction in (DIR_X, DIR_Y, DIR_Z):
        total = None
        for q in range(19):
            if direction[q] == 0:
                continue
            term = fields[q] if direction[q] > 0 else -fields[q]
            total = term if total is None else total + term
        moments.append(total)
    vel = [m * scale for m in moments]
    square = vel[0] * vel[0] + vel[1] * vel[1] + vel[2] * vel[2]
    weighted_sum = None
    density_part = None
    dv = [None, None, None]
    for q in range(19):
        weighted = (RELAX_RATE * float(WEIGHTS[q])) * cots[q]
        weighted_sum = weighted if weighted_sum is None else weighted_sum + weighted
        along = None
        for sign, v in zip((DIR_X[q], DIR_Y[q], DIR_Z[q]), vel):
            if sign == 0:
                continue
            term = v if sign > 0 else -v
            along = term if along is None else along + term
        if along is None:
            shape = 1.0 - 1.5 * square
        else:
            shape = 1.0 + along * (3.0 + 4.5 * along) - 1.5 * square
            slope = weighted * (3.0 + 9.0 * along)
            for axis, sign in enumerate((DIR_X[q], DIR_Y[q], DIR_Z[q])):
                if sign == 0:
                    continue
                term = slope if sign > 0 else -slope
                dv[axis] = term if dv[axis] is None else dv[axis] + term
        part = weighted * shape
        density_part = part if density_part is None else density_part + part
    dv = [density * (d - 3.0 * v * weighted_sum) for d, v in zip(dv, vel)]
    through = (moments[0] * dv[0] + moments[1] * dv[1] + moments[2] * dv[2]) * recip
    common = density_part - scale * through
    scaled = [scale * d for d in dv]
    grads = []
    for q in range(19):
        grad = (1.0 - RELAX_RATE) * cots[q] + common
        for sign, d in zip((DIR_X[q], DIR_Y[q], DIR_Z[q]), scaled):
            if sign == 0:
                continue
            grad = grad + d if sign > 0 else grad - d
        grads.append(grad)
    return grads, -through


def plane_list(q_count, layers):
    planes = [(0, q, z) for q in range(q_count) for z in range(layers)]
    planes += [(1, q, z) for q in range(q_count) for z in range(layers)]
    planes += [(2, 0, z) for z in range(layers)]
    return planes


def pack_kernel(f_ref, cot_ref, porosity_ref, ids_ref, slot_ref, packed_ref, solid_ref, tile_ref):
    q_count, layers, height, width = f_ref.shape
    groups = packed_ref.shape[0]
    for b in range(layers * height):
        tile_ref[b] = jnp.float32(0.0)
    for n in range(ids_ref.shape[0]):
        brick = ids_ref[n]
        tile_ref[brick] = tile_ref[brick] + porosity_ref[slot_ref[n]]
    for z in range(layers):
        for y in range(height):
            solid_ref[z, y : y + 1, :] = jnp.full((1, width), tile_ref[z * height + y], jnp.float32)
    lane = lax.broadcasted_iota(jnp.int32, (height, width), 1)
    zero = jnp.zeros((height, width), jnp.float32)
    acc = [zero for g in range(groups)]
    for index, (field, q, z) in enumerate(plane_list(q_count, layers)):
        if field == 0:
            own = f_ref[q, z]
        elif field == 1:
            own = cot_ref[q, z].astype(jnp.float32)
        else:
            own = solid_ref[z]
        group, slot = divmod(index, width // 4)
        mine = (lane >= 4 * slot) & (lane < 4 * slot + 4)
        acc[group] = jnp.where(mine, pltpu.roll(own, (4 * slot - (width - 2)) % width, 1), acc[group])
    for g in range(groups):
        packed_ref[g] = acc[g]


def compute_kernel(f_hbm, cot_hbm, solid_ref, up_ref, dn_ref, from_left_ref, from_right_ref,
                   grad_ref, sbar_ref, ef, ec, es, cf, bo, sb2, f_ref, cot_ref, sems):
    q_count, layers, height, width = f_ref.shape
    groups = from_left_ref.shape[0]
    corner_base = (2 * q_count + 1) * layers * 2
    f_copy = pltpu.make_async_copy(f_hbm, f_ref, sems.at[0])
    cot_copy = pltpu.make_async_copy(cot_hbm, cot_ref, sems.at[1])
    f_copy.start()
    cot_copy.start()
    lane_own = lax.broadcasted_iota(jnp.int32, (height, width), 1)
    lane_edge = lax.broadcasted_iota(jnp.int32, (2, width), 1)
    tail = ROWS - (TOP + height + 2)

    def sides(left, right, slot, lane):
        from_r = pltpu.roll(right, (-(4 * slot + 2)) % width, 1)
        from_l = pltpu.roll(left, (width - 2 - 4 * slot) % width, 1)
        return jnp.where(lane < 2, from_r, jnp.where(lane >= width - 2, from_l, 0.0))

    def place_halo(target, index, row_index, z):
        group, slot = divmod(index, width // 4)
        base = (row_index * layers + z) * 2
        left_rows = corner_base + 2 * group
        right_rows = corner_base + 2 * (groups + group)
        target[TOP : TOP + height, width:LANES] = sides(
            from_left_ref[group], from_right_ref[group], slot, lane_own)
        target[0:TOP, width:LANES] = sides(
            up_ref[left_rows : left_rows + 2], up_ref[right_rows : right_rows + 2], slot, lane_edge)
        target[TOP + height : TOP + height + 2, width:LANES] = sides(
            dn_ref[left_rows : left_rows + 2], dn_ref[right_rows : right_rows + 2], slot, lane_edge)
        target[TOP + height + 2 : ROWS, :] = jnp.zeros((tail, LANES), jnp.float32)
        target[0:TOP, 0:width] = up_ref[base : base + 2]
        target[TOP + height : TOP + height + 2, 0:width] = dn_ref[base : base + 2]

    targets = []
    for index, (field, q, z) in enumerate(plane_list(q_count, layers)):
        row_index = field * q_count + q
        target = (ef.at[q, z], ec.at[q, z], es.at[z])[field]
        place_halo(target, index, row_index, z)
        targets.append((field, q, z, target))
    f_copy.wait()
    cot_copy.wait()
    for field, q, z, target in targets:
        if field == 0:
            own = f_ref[q, z]
        elif field == 1:
            own = cot_ref[q, z].astype(jnp.float32)
        else:
            own = solid_ref[z]
        target[TOP : TOP + height, 0:width] = own

    def phase_one(z, carry):
        for k in range((TOP + height + 2 + 7) // 8):
            rows = pl.ds(8 * k, 8)
            out = collide([ef[q, z, rows, :] for q in range(q_count)], es[z, rows, :])
            for q in range(q_count):
                cf[q, z, rows, :] = out[q]
        return carry

    lax.fori_loop(0, layers, phase_one, 0)

    def phase_two(z, carry):
        for k in range((ROWS - 8) // 8):
            start = TOP - 1 + 8 * k
            moved = []
            back = []
            for q in range(q_count):
                ex, ey, ez = int(DIR_X[q]), int(DIR_Y[q]), int(DIR_Z[q])
                src = cf[q, (z - ez + layers) % layers, pl.ds(start - ey, 8), :]
                moved.append(pltpu.roll(src, ex % LANES, 1) if ex else src)
                src = ec[q, (z + ez) % layers, pl.ds(start + ey, 8), :]
                back.append(pltpu.roll(src, (-ex) % LANES, 1) if ex else src)
            grad_field, grad_solid = collide_vjp(moved, es[z, pl.ds(start, 8), :], back)
            for q in range(q_count):
                bo[q, z, pl.ds(8 * k, 8), :] = grad_field[q]
            sb2[z, pl.ds(8 * k, 8), :] = grad_solid
        return carry

    lax.fori_loop(0, layers, phase_two, 0)

    def phase_three(z, carry):
        for k in range(height // 8):
            rows = pl.ds(8 * k, 8)
            pulled = []
            for q in range(q_count):
                ex, ey, ez = int(DIR_X[q]), int(DIR_Y[q]), int(DIR_Z[q])
                src = bo[q, (z + ez) % layers, pl.ds(1 + ey + 8 * k, 8), :]
                if ex:
                    src = pltpu.roll(src, (-ex) % LANES, 1)
                pulled.append(src[:, 0:width])
            field = [f_ref[q, z, rows, :] for q in range(q_count)]
            grad_field, grad_solid = collide_vjp(field, solid_ref[z, rows, :], pulled)
            for q in range(q_count):
                grad_ref[q, z, rows, :] = grad_field[q]
            sbar_ref[z, rows, :] = grad_solid + sb2[z, pl.ds(1 + 8 * k, 8), 0:width]
        return carry

    lax.fori_loop(0, layers, phase_three, 0)


def vmem_specs(count):
    return [pl.BlockSpec(memory_space=pltpu.VMEM) for _ in range(count)]


def on_device(f_start, cotangent, porosity, brick_ids, brick_slot):
    q_count, layers_dev, rows_dev, cols_dev = f_start.shape
    nx = lax.axis_size("gx")
    ny = lax.axis_size("gy")
    tile_count = cols_dev // 128
    brick_count = layers_dev * rows_dev * tile_count
    listed = brick_ids.reshape(-1)
    slots_of = brick_slot.reshape(-1)
    slot_table = porosity.reshape(-1)
    brick_hit = (listed[:, None] == jnp.arange(brick_count, dtype=jnp.int32)[None, :]).astype(
        jnp.float32
    )
    slot_hit = (
        slots_of[:, None] == jnp.arange(slot_table.shape[0], dtype=jnp.int32)[None, :]
    ).astype(jnp.float32)

    def shift(value, axis, size, step):
        return lax.ppermute(value, axis, [(i, (i + step) % size) for i in range(size)])

    cot32 = cotangent.astype(jnp.float32)
    plane_count = (2 * q_count + 1) * layers_dev
    groups = -(-plane_count // (cols_dev // 4))
    smem = pl.BlockSpec(memory_space=pltpu.SMEM)
    packed, solid = pl.pallas_call(
        pack_kernel,
        out_shape=(
            jax.ShapeDtypeStruct((groups, rows_dev, cols_dev), jnp.float32),
            jax.ShapeDtypeStruct((layers_dev, rows_dev, cols_dev), jnp.float32),
        ),
        in_specs=vmem_specs(2) + [smem, smem, smem],
        out_specs=tuple(vmem_specs(2)),
        scratch_shapes=[pltpu.SMEM((brick_count,), jnp.float32)],
    )(f_start, cotangent, slot_table, listed, slots_of)
    from_left = shift(packed, "gx", nx, 1)
    from_right = shift(packed, "gx", nx, -1)

    def edge_rows(chosen):
        rows = jnp.concatenate([f_start[:, :, chosen], cot32[:, :, chosen], solid[None, :, chosen]], axis=0)
        corners = jnp.concatenate([from_left[:, chosen], from_right[:, chosen]], axis=0)
        return jnp.concatenate(
            [rows.reshape(-1, cols_dev), corners.reshape(-1, cols_dev)], axis=0
        )

    first_rows = edge_rows(slice(0, 2))
    last_rows = edge_rows(slice(rows_dev - 2, rows_dev))
    up_rows = shift(last_rows, "gy", ny, 1)
    dn_rows = shift(first_rows, "gy", ny, -1)
    big = pltpu.VMEM((q_count, layers_dev, ROWS, LANES), jnp.float32)
    start_grad, solid_bar = pl.pallas_call(
        compute_kernel,
        out_shape=(
            jax.ShapeDtypeStruct(f_start.shape, jnp.float32),
            jax.ShapeDtypeStruct(solid.shape, jnp.float32),
        ),
        in_specs=[pl.BlockSpec(memory_space=pl.ANY)] * 2 + vmem_specs(5),
        out_specs=tuple(vmem_specs(2)),
        scratch_shapes=[
            big,
            big,
            pltpu.VMEM((layers_dev, ROWS, LANES), jnp.float32),
            big,
            pltpu.VMEM((q_count, layers_dev, ROWS - 8, LANES), jnp.float32),
            pltpu.VMEM((layers_dev, ROWS - 8, LANES), jnp.float32),
            pltpu.VMEM(f_start.shape, jnp.float32),
            pltpu.VMEM(cotangent.shape, cotangent.dtype),
            pltpu.SemaphoreType.DMA((2,)),
        ],
        compiler_params=pltpu.CompilerParams(vmem_limit_bytes=48 * 1024 * 1024),
    )(f_start, cotangent, solid, up_rows, dn_rows, from_left, from_right)
    tile_sums = jnp.sum(solid_bar.reshape(brick_count, 128), axis=1)
    brick_sum = jnp.sum(brick_hit * tile_sums[None, :], axis=1)
    slot_grad = jnp.sum(slot_hit * brick_sum[:, None], axis=0)
    return (start_grad, slot_grad.reshape(porosity.shape))


def solution(mesh):
    return jax.shard_map(
        on_device,
        mesh=mesh,
        in_specs=(
            P(None, None, "gy", "gx"),
            P(None, None, "gy", "gx"),
            P("gx", "gy", None),
            P("gx", "gy", None),
            P("gx", "gy", None),
        ),
        out_specs=(P(None, None, "gy", "gx"), P("gx", "gy", None)),
        check_vma=False,
    )
```

```python
import jax
import jax.numpy as jnp
import numpy as np
from jax import lax
from jax.experimental import pallas as pl
from jax.experimental.pallas import tpu as pltpu
from jax.sharding import PartitionSpec as P

DIR_X = np.array([0, 1, -1, 0, 0, 0, 0, 1, -1, 1, -1, 1, -1, 1, -1, 0, 0, 0, 0])
DIR_Y = np.array([0, 0, 0, 1, -1, 0, 0, 1, 1, -1, -1, 0, 0, 0, 0, 1, -1, 1, -1])
DIR_Z = np.array([0, 0, 0, 0, 0, 1, -1, 0, 0, 0, 0, 1, 1, -1, -1, 1, 1, -1, -1])
WEIGHTS = np.array([1.0 / 3.0] + [1.0 / 18.0] * 6 + [1.0 / 36.0] * 12)
RELAX_RATE = 0.8

ROWS = 48
LANES = 256
TOP = 2


def collide(fields, solid):
    density = fields[0]
    for value in fields[1:]:
        density = density + value
    inverse = (1.0 - solid) / density
    moments = []
    for direction in (DIR_X, DIR_Y, DIR_Z):
        total = None
        for q in range(19):
            if direction[q] == 0:
                continue
            term = fields[q] if direction[q] > 0 else -fields[q]
            total = term if total is None else total + term
        moments.append(total * inverse)
    vel_x, vel_y, vel_z = moments
    square = vel_x * vel_x + vel_y * vel_y + vel_z * vel_z
    out = []
    for q in range(19):
        along = None
        for sign, vel in ((DIR_X[q], vel_x), (DIR_Y[q], vel_y), (DIR_Z[q], vel_z)):
            if sign == 0:
                continue
            term = vel if sign > 0 else -vel
            along = term if along is None else along + term
        if along is None:
            shape = 1.0 - 1.5 * square
        else:
            shape = 1.0 + 3.0 * along + 4.5 * along * along - 1.5 * square
        balance = float(WEIGHTS[q]) * density * shape
        out.append(fields[q] - RELAX_RATE * (fields[q] - balance))
    return out


def collide_vjp(fields, solid, cots):
    density = fields[0]
    for value in fields[1:]:
        density = density + value
    recip = 1.0 / density
    scale = (1.0 - solid) * recip
    moments = []
    for direction in (DIR_X, DIR_Y, DIR_Z):
        total = None
        for q in range(19):
            if direction[q] == 0:
                continue
            term = fields[q] if direction[q] > 0 else -fields[q]
            total = term if total is None else total + term
        moments.append(total)
    vel = [m * scale for m in moments]
    square = vel[0] * vel[0] + vel[1] * vel[1] + vel[2] * vel[2]
    weighted_sum = None
    density_part = None
    dv = [None, None, None]
    for q in range(19):
        weighted = (RELAX_RATE * float(WEIGHTS[q])) * cots[q]
        weighted_sum = weighted if weighted_sum is None else weighted_sum + weighted
        along = None
        for sign, v in zip((DIR_X[q], DIR_Y[q], DIR_Z[q]), vel):
            if sign == 0:
                continue
            term = v if sign > 0 else -v
            along = term if along is None else along + term
        if along is None:
            shape = 1.0 - 1.5 * square
        else:
            shape = 1.0 + along * (3.0 + 4.5 * along) - 1.5 * square
            slope = weighted * (3.0 + 9.0 * along)
            for axis, sign in enumerate((DIR_X[q], DIR_Y[q], DIR_Z[q])):
                if sign == 0:
                    continue
                term = slope if sign > 0 else -slope
                dv[axis] = term if dv[axis] is None else dv[axis] + term
        part = weighted * shape
        density_part = part if density_part is None else density_part + part
    dv = [density * (d - 3.0 * v * weighted_sum) for d, v in zip(dv, vel)]
    through = (moments[0] * dv[0] + moments[1] * dv[1] + moments[2] * dv[2]) * recip
    common = density_part - scale * through
    scaled = [scale * d for d in dv]
    grads = []
    for q in range(19):
        grad = (1.0 - RELAX_RATE) * cots[q] + common
        for sign, d in zip((DIR_X[q], DIR_Y[q], DIR_Z[q]), scaled):
            if sign == 0:
                continue
            grad = grad + d if sign > 0 else grad - d
        grads.append(grad)
    return grads, -through


def plane_list(q_count, layers):
    planes = [(0, q, z) for q in range(q_count) for z in range(layers)]
    planes += [(1, q, z) for q in range(q_count) for z in range(layers)]
    planes += [(2, 0, z) for z in range(layers)]
    return planes


def pack_kernel(f_ref, cot_ref, porosity_ref, ids_ref, slot_ref, packed_ref, solid_ref, tile_ref):
    q_count, layers, height, width = f_ref.shape
    groups = packed_ref.shape[0]
    for b in range(layers * height):
        tile_ref[b] = jnp.float32(0.0)
    for n in range(ids_ref.shape[0]):
        brick = ids_ref[n]
        tile_ref[brick] = tile_ref[brick] + porosity_ref[slot_ref[n]]
    for z in range(layers):
        for y in range(height):
            solid_ref[z, y : y + 1, :] = jnp.full((1, width), tile_ref[z * height + y], jnp.float32)
    lane = lax.broadcasted_iota(jnp.int32, (height, width), 1)
    zero = jnp.zeros((height, width), jnp.float32)
    acc = [zero for g in range(groups)]
    for index, (field, q, z) in enumerate(plane_list(q_count, layers)):
        if field == 0:
            own = f_ref[q, z]
        elif field == 1:
            own = cot_ref[q, z].astype(jnp.float32)
        else:
            own = solid_ref[z]
        group, slot = divmod(index, width // 4)
        mine = (lane >= 4 * slot) & (lane < 4 * slot + 4)
        acc[group] = jnp.where(mine, pltpu.roll(own, (4 * slot - (width - 2)) % width, 1), acc[group])
    for g in range(groups):
        packed_ref[g] = acc[g]


def compute_kernel(f_hbm, cot_hbm, solid_ref, up_ref, dn_ref, from_left_ref, from_right_ref,
                   grad_ref, sbar_ref, ef, ec, es, cf, bo, sb2, f_ref, cot_ref, sems):
    q_count, layers, height, width = f_ref.shape
    groups = from_left_ref.shape[0]
    corner_base = (2 * q_count + 1) * layers * 2
    f_copy = pltpu.make_async_copy(f_hbm, f_ref, sems.at[0])
    cot_copy = pltpu.make_async_copy(cot_hbm, cot_ref, sems.at[1])
    f_copy.start()
    cot_copy.start()
    lane_own = lax.broadcasted_iota(jnp.int32, (height, width), 1)
    lane_edge = lax.broadcasted_iota(jnp.int32, (2, width), 1)
    tail = ROWS - (TOP + height + 2)

    def sides(left, right, slot, lane):
        from_r = pltpu.roll(right, (-(4 * slot + 2)) % width, 1)
        from_l = pltpu.roll(left, (width - 2 - 4 * slot) % width, 1)
        return jnp.where(lane < 2, from_r, jnp.where(lane >= width - 2, from_l, 0.0))

    def place_halo(target, index, row_index, z):
        group, slot = divmod(index, width // 4)
        base = (row_index * layers + z) * 2
        left_rows = corner_base + 2 * group
        right_rows = corner_base + 2 * (groups + group)
        target[TOP : TOP + height, width:LANES] = sides(
            from_left_ref[group], from_right_ref[group], slot, lane_own)
        target[0:TOP, width:LANES] = sides(
            up_ref[left_rows : left_rows + 2], up_ref[right_rows : right_rows + 2], slot, lane_edge)
        target[TOP + height : TOP + height + 2, width:LANES] = sides(
            dn_ref[left_rows : left_rows + 2], dn_ref[right_rows : right_rows + 2], slot, lane_edge)
        target[TOP + height + 2 : ROWS, :] = jnp.zeros((tail, LANES), jnp.float32)
        target[0:TOP, 0:width] = up_ref[base : base + 2]
        target[TOP + height : TOP + height + 2, 0:width] = dn_ref[base : base + 2]

    targets = []
    for index, (field, q, z) in enumerate(plane_list(q_count, layers)):
        row_index = field * q_count + q
        target = (ef.at[q, z], ec.at[q, z], es.at[z])[field]
        place_halo(target, index, row_index, z)
        targets.append((field, q, z, target))
    f_copy.wait()
    cot_copy.wait()
    for field, q, z, target in targets:
        if field == 0:
            own = f_ref[q, z]
        elif field == 1:
            own = cot_ref[q, z].astype(jnp.float32)
        else:
            own = solid_ref[z]
        target[TOP : TOP + height, 0:width] = own

    def phase_one(z, carry):
        for k in range((TOP + height + 2 + 7) // 8):
            rows = pl.ds(8 * k, 8)
            out = collide([ef[q, z, rows, :] for q in range(q_count)], es[z, rows, :])
            for q in range(q_count):
                cf[q, z, rows, :] = out[q]
        return carry

    lax.fori_loop(0, layers, phase_one, 0, unroll=True)

    def phase_two(z, carry):
        for k in range((ROWS - 8) // 8):
            start = TOP - 1 + 8 * k
            moved = []
            back = []
            for q in range(q_count):
                ex, ey, ez = int(DIR_X[q]), int(DIR_Y[q]), int(DIR_Z[q])
                src = cf[q, (z - ez + layers) % layers, pl.ds(start - ey, 8), :]
                moved.append(pltpu.roll(src, ex % LANES, 1) if ex else src)
                src = ec[q, (z + ez) % layers, pl.ds(start + ey, 8), :]
                back.append(pltpu.roll(src, (-ex) % LANES, 1) if ex else src)
            grad_field, grad_solid = collide_vjp(moved, es[z, pl.ds(start, 8), :], back)
            for q in range(q_count):
                bo[q, z, pl.ds(8 * k, 8), :] = grad_field[q]
            sb2[z, pl.ds(8 * k, 8), :] = grad_solid
        return carry

    lax.fori_loop(0, layers, phase_two, 0, unroll=True)

    def phase_three(z, carry):
        for k in range(height // 8):
            rows = pl.ds(8 * k, 8)
            pulled = []
            for q in range(q_count):
                ex, ey, ez = int(DIR_X[q]), int(DIR_Y[q]), int(DIR_Z[q])
                src = bo[q, (z + ez) % layers, pl.ds(1 + ey + 8 * k, 8), :]
                if ex:
                    src = pltpu.roll(src, (-ex) % LANES, 1)
                pulled.append(src[:, 0:width])
            field = [f_ref[q, z, rows, :] for q in range(q_count)]
            grad_field, grad_solid = collide_vjp(field, solid_ref[z, rows, :], pulled)
            for q in range(q_count):
                grad_ref[q, z, rows, :] = grad_field[q]
            sbar_ref[z, rows, :] = grad_solid + sb2[z, pl.ds(1 + 8 * k, 8), 0:width]
        return carry

    lax.fori_loop(0, layers, phase_three, 0, unroll=True)


def vmem_specs(count):
    return [pl.BlockSpec(memory_space=pltpu.VMEM) for _ in range(count)]


def on_device(f_start, cotangent, porosity, brick_ids, brick_slot):
    q_count, layers_dev, rows_dev, cols_dev = f_start.shape
    nx = lax.axis_size("gx")
    ny = lax.axis_size("gy")
    tile_count = cols_dev // 128
    brick_count = layers_dev * rows_dev * tile_count
    listed = brick_ids.reshape(-1)
    slots_of = brick_slot.reshape(-1)
    slot_table = porosity.reshape(-1)
    brick_hit = (listed[:, None] == jnp.arange(brick_count, dtype=jnp.int32)[None, :]).astype(
        jnp.float32
    )
    slot_hit = (
        slots_of[:, None] == jnp.arange(slot_table.shape[0], dtype=jnp.int32)[None, :]
    ).astype(jnp.float32)

    def shift(value, axis, size, step):
        return lax.ppermute(value, axis, [(i, (i + step) % size) for i in range(size)])

    cot32 = cotangent.astype(jnp.float32)
    plane_count = (2 * q_count + 1) * layers_dev
    groups = -(-plane_count // (cols_dev // 4))
    smem = pl.BlockSpec(memory_space=pltpu.SMEM)
    packed, solid = pl.pallas_call(
        pack_kernel,
        out_shape=(
            jax.ShapeDtypeStruct((groups, rows_dev, cols_dev), jnp.float32),
            jax.ShapeDtypeStruct((layers_dev, rows_dev, cols_dev), jnp.float32),
        ),
        in_specs=vmem_specs(2) + [smem, smem, smem],
        out_specs=tuple(vmem_specs(2)),
        scratch_shapes=[pltpu.SMEM((brick_count,), jnp.float32)],
    )(f_start, cotangent, slot_table, listed, slots_of)
    from_left = shift(packed, "gx", nx, 1)
    from_right = shift(packed, "gx", nx, -1)

    def edge_rows(chosen):
        rows = jnp.concatenate([f_start[:, :, chosen], cot32[:, :, chosen], solid[None, :, chosen]], axis=0)
        corners = jnp.concatenate([from_left[:, chosen], from_right[:, chosen]], axis=0)
        return jnp.concatenate(
            [rows.reshape(-1, cols_dev), corners.reshape(-1, cols_dev)], axis=0
        )

    first_rows = edge_rows(slice(0, 2))
    last_rows = edge_rows(slice(rows_dev - 2, rows_dev))
    up_rows = shift(last_rows, "gy", ny, 1)
    dn_rows = shift(first_rows, "gy", ny, -1)
    big = pltpu.VMEM((q_count, layers_dev, ROWS, LANES), jnp.float32)
    start_grad, solid_bar = pl.pallas_call(
        compute_kernel,
        out_shape=(
            jax.ShapeDtypeStruct(f_start.shape, jnp.float32),
            jax.ShapeDtypeStruct(solid.shape, jnp.float32),
        ),
        in_specs=[pl.BlockSpec(memory_space=pl.ANY)] * 2 + vmem_specs(5),
        out_specs=tuple(vmem_specs(2)),
        scratch_shapes=[
            big,
            big,
            pltpu.VMEM((layers_dev, ROWS, LANES), jnp.float32),
            big,
            pltpu.VMEM((q_count, layers_dev, ROWS - 8, LANES), jnp.float32),
            pltpu.VMEM((layers_dev, ROWS - 8, LANES), jnp.float32),
            pltpu.VMEM(f_start.shape, jnp.float32),
            pltpu.VMEM(cotangent.shape, cotangent.dtype),
            pltpu.SemaphoreType.DMA((2,)),
        ],
        compiler_params=pltpu.CompilerParams(vmem_limit_bytes=48 * 1024 * 1024),
    )(f_start, cotangent, solid, up_rows, dn_rows, from_left, from_right)
    tile_sums = jnp.sum(solid_bar.reshape(brick_count, 128), axis=1)
    brick_sum = jnp.sum(brick_hit * tile_sums[None, :], axis=1)
    slot_grad = jnp.sum(slot_hit * brick_sum[:, None], axis=0)
    return (start_grad, slot_grad.reshape(porosity.shape))


def solution(mesh):
    return jax.shard_map(
        on_device,
        mesh=mesh,
        in_specs=(
            P(None, None, "gy", "gx"),
            P(None, None, "gy", "gx"),
            P("gx", "gy", None),
            P("gx", "gy", None),
            P("gx", "gy", None),
        ),
        out_specs=(P(None, None, "gy", "gx"), P("gx", "gy", None)),
        check_vma=False,
    )
```

```python
import jax
import jax.numpy as jnp
import numpy as np
from jax import lax
from jax.experimental import pallas as pl
from jax.experimental.pallas import tpu as pltpu
from jax.sharding import PartitionSpec as P

DIR_X = np.array([0, 1, -1, 0, 0, 0, 0, 1, -1, 1, -1, 1, -1, 1, -1, 0, 0, 0, 0])
DIR_Y = np.array([0, 0, 0, 1, -1, 0, 0, 1, 1, -1, -1, 0, 0, 0, 0, 1, -1, 1, -1])
DIR_Z = np.array([0, 0, 0, 0, 0, 1, -1, 0, 0, 0, 0, 1, 1, -1, -1, 1, 1, -1, -1])
WEIGHTS = np.array([1.0 / 3.0] + [1.0 / 18.0] * 6 + [1.0 / 36.0] * 12)
RELAX_RATE = 0.8

ROWS = 48
LANES = 256
TOP = 2


def collide(fields, solid):
    density = fields[0]
    for value in fields[1:]:
        density = density + value
    inverse = (1.0 - solid) / density
    moments = []
    for direction in (DIR_X, DIR_Y, DIR_Z):
        total = None
        for q in range(19):
            if direction[q] == 0:
                continue
            term = fields[q] if direction[q] > 0 else -fields[q]
            total = term if total is None else total + term
        moments.append(total * inverse)
    vel_x, vel_y, vel_z = moments
    square = vel_x * vel_x + vel_y * vel_y + vel_z * vel_z
    out = []
    for q in range(19):
        along = None
        for sign, vel in ((DIR_X[q], vel_x), (DIR_Y[q], vel_y), (DIR_Z[q], vel_z)):
            if sign == 0:
                continue
            term = vel if sign > 0 else -vel
            along = term if along is None else along + term
        if along is None:
            shape = 1.0 - 1.5 * square
        else:
            shape = 1.0 + 3.0 * along + 4.5 * along * along - 1.5 * square
        balance = float(WEIGHTS[q]) * density * shape
        out.append(fields[q] - RELAX_RATE * (fields[q] - balance))
    return out


def collide_vjp(fields, solid, cots):
    density = fields[0]
    for value in fields[1:]:
        density = density + value
    recip = 1.0 / density
    scale = (1.0 - solid) * recip
    moments = []
    for direction in (DIR_X, DIR_Y, DIR_Z):
        total = None
        for q in range(19):
            if direction[q] == 0:
                continue
            term = fields[q] if direction[q] > 0 else -fields[q]
            total = term if total is None else total + term
        moments.append(total)
    vel = [m * scale for m in moments]
    square = vel[0] * vel[0] + vel[1] * vel[1] + vel[2] * vel[2]
    weighted_sum = None
    density_part = None
    dv = [None, None, None]
    for q in range(19):
        weighted = (RELAX_RATE * float(WEIGHTS[q])) * cots[q]
        weighted_sum = weighted if weighted_sum is None else weighted_sum + weighted
        along = None
        for sign, v in zip((DIR_X[q], DIR_Y[q], DIR_Z[q]), vel):
            if sign == 0:
                continue
            term = v if sign > 0 else -v
            along = term if along is None else along + term
        if along is None:
            shape = 1.0 - 1.5 * square
        else:
            shape = 1.0 + along * (3.0 + 4.5 * along) - 1.5 * square
            slope = weighted * (3.0 + 9.0 * along)
            for axis, sign in enumerate((DIR_X[q], DIR_Y[q], DIR_Z[q])):
                if sign == 0:
                    continue
                term = slope if sign > 0 else -slope
                dv[axis] = term if dv[axis] is None else dv[axis] + term
        part = weighted * shape
        density_part = part if density_part is None else density_part + part
    dv = [density * (d - 3.0 * v * weighted_sum) for d, v in zip(dv, vel)]
    through = (moments[0] * dv[0] + moments[1] * dv[1] + moments[2] * dv[2]) * recip
    common = density_part - scale * through
    scaled = [scale * d for d in dv]
    grads = []
    for q in range(19):
        grad = (1.0 - RELAX_RATE) * cots[q] + common
        for sign, d in zip((DIR_X[q], DIR_Y[q], DIR_Z[q]), scaled):
            if sign == 0:
                continue
            grad = grad + d if sign > 0 else grad - d
        grads.append(grad)
    return grads, -through


def plane_list(q_count, layers):
    planes = [(0, q, z) for q in range(q_count) for z in range(layers)]
    planes += [(1, q, z) for q in range(q_count) for z in range(layers)]
    planes += [(2, 0, z) for z in range(layers)]
    return planes


def pack_kernel(f_ref, cot_ref, porosity_ref, ids_ref, slot_ref, packed_ref, solid_ref, tile_ref):
    q_count, layers, height, width = f_ref.shape
    groups = packed_ref.shape[0]
    for b in range(layers * height):
        tile_ref[b] = jnp.float32(0.0)
    for n in range(ids_ref.shape[0]):
        brick = ids_ref[n]
        tile_ref[brick] = tile_ref[brick] + porosity_ref[slot_ref[n]]
    for z in range(layers):
        for y in range(height):
            solid_ref[z, y : y + 1, :] = jnp.full((1, width), tile_ref[z * height + y], jnp.float32)
    lane = lax.broadcasted_iota(jnp.int32, (height, width), 1)
    zero = jnp.zeros((height, width), jnp.float32)
    acc = [zero for g in range(groups)]
    for index, (field, q, z) in enumerate(plane_list(q_count, layers)):
        if field == 0:
            own = f_ref[q, z]
        elif field == 1:
            own = cot_ref[q, z].astype(jnp.float32)
        else:
            own = solid_ref[z]
        group, slot = divmod(index, width // 4)
        mine = (lane >= 4 * slot) & (lane < 4 * slot + 4)
        acc[group] = jnp.where(mine, pltpu.roll(own, (4 * slot - (width - 2)) % width, 1), acc[group])
    for g in range(groups):
        packed_ref[g] = acc[g]


def compute_kernel(f_hbm, cot_hbm, solid_ref, up_ref, dn_ref, from_left_ref, from_right_ref,
                   grad_ref, sbar_ref, ef, ec, es, cf, bo, sb2, f_ref, cot_ref, sems):
    q_count, layers, height, width = f_ref.shape
    groups = from_left_ref.shape[0]
    corner_base = (2 * q_count + 1) * layers * 2
    f_copy = pltpu.make_async_copy(f_hbm, f_ref, sems.at[0])
    cot_copy = pltpu.make_async_copy(cot_hbm, cot_ref, sems.at[1])
    f_copy.start()
    cot_copy.start()
    lane_own = lax.broadcasted_iota(jnp.int32, (height, width), 1)
    lane_edge = lax.broadcasted_iota(jnp.int32, (2, width), 1)
    tail = ROWS - (TOP + height + 2)

    def sides(left, right, slot, lane):
        from_r = pltpu.roll(right, (-(4 * slot + 2)) % width, 1)
        from_l = pltpu.roll(left, (width - 2 - 4 * slot) % width, 1)
        return jnp.where(lane < 2, from_r, jnp.where(lane >= width - 2, from_l, 0.0))

    def place_halo(target, index, row_index, z):
        group, slot = divmod(index, width // 4)
        base = (row_index * layers + z) * 2
        left_rows = corner_base + 2 * group
        right_rows = corner_base + 2 * (groups + group)
        target[TOP : TOP + height, width:LANES] = sides(
            from_left_ref[group], from_right_ref[group], slot, lane_own)
        target[0:TOP, width:LANES] = sides(
            up_ref[left_rows : left_rows + 2], up_ref[right_rows : right_rows + 2], slot, lane_edge)
        target[TOP + height : TOP + height + 2, width:LANES] = sides(
            dn_ref[left_rows : left_rows + 2], dn_ref[right_rows : right_rows + 2], slot, lane_edge)
        target[0:TOP, 0:width] = up_ref[base : base + 2]
        target[TOP + height : TOP + height + 2, 0:width] = dn_ref[base : base + 2]

    targets = []
    for index, (field, q, z) in enumerate(plane_list(q_count, layers)):
        row_index = field * q_count + q
        target = (ef.at[q, z], ec.at[q, z], es.at[z])[field]
        place_halo(target, index, row_index, z)
        targets.append((field, q, z, target))
    f_copy.wait()
    cot_copy.wait()
    for field, q, z, target in targets:
        if field == 0:
            own = f_ref[q, z]
        elif field == 1:
            own = cot_ref[q, z].astype(jnp.float32)
        else:
            own = solid_ref[z]
        target[TOP : TOP + height, 0:width] = own

    def phase_one(z, carry):
        for k in range((TOP + height + 2 + 7) // 8):
            rows = pl.ds(8 * k, 8)
            out = collide([ef[q, z, rows, :] for q in range(q_count)], es[z, rows, :])
            for q in range(q_count):
                cf[q, z, rows, :] = out[q]
        return carry

    lax.fori_loop(0, layers, phase_one, 0)

    def phase_two(z, carry):
        for k in range((ROWS - 8) // 8):
            start = TOP - 1 + 8 * k
            moved = []
            back = []
            for q in range(q_count):
                ex, ey, ez = int(DIR_X[q]), int(DIR_Y[q]), int(DIR_Z[q])
                src = cf[q, (z - ez + layers) % layers, pl.ds(start - ey, 8), :]
                moved.append(pltpu.roll(src, ex % LANES, 1) if ex else src)
                src = ec[q, (z + ez) % layers, pl.ds(start + ey, 8), :]
                back.append(pltpu.roll(src, (-ex) % LANES, 1) if ex else src)
            grad_field, grad_solid = collide_vjp(moved, es[z, pl.ds(start, 8), :], back)
            for q in range(q_count):
                bo[q, z, pl.ds(8 * k, 8), :] = grad_field[q]
            sb2[z, pl.ds(8 * k, 8), :] = grad_solid
        return carry

    lax.fori_loop(0, layers, phase_two, 0)

    def phase_three(z, carry):
        for k in range(height // 8):
            rows = pl.ds(8 * k, 8)
            pulled = []
            for q in range(q_count):
                ex, ey, ez = int(DIR_X[q]), int(DIR_Y[q]), int(DIR_Z[q])
                src = bo[q, (z + ez) % layers, pl.ds(1 + ey + 8 * k, 8), :]
                if ex:
                    src = pltpu.roll(src, (-ex) % LANES, 1)
                pulled.append(src[:, 0:width])
            field = [f_ref[q, z, rows, :] for q in range(q_count)]
            grad_field, grad_solid = collide_vjp(field, solid_ref[z, rows, :], pulled)
            for q in range(q_count):
                grad_ref[q, z, rows, :] = grad_field[q]
            sbar_ref[z, rows, :] = grad_solid + sb2[z, pl.ds(1 + 8 * k, 8), 0:width]
        return carry

    lax.fori_loop(0, layers, phase_three, 0)


def vmem_specs(count):
    return [pl.BlockSpec(memory_space=pltpu.VMEM) for _ in range(count)]


def on_device(f_start, cotangent, porosity, brick_ids, brick_slot):
    q_count, layers_dev, rows_dev, cols_dev = f_start.shape
    nx = lax.axis_size("gx")
    ny = lax.axis_size("gy")
    tile_count = cols_dev // 128
    brick_count = layers_dev * rows_dev * tile_count
    listed = brick_ids.reshape(-1)
    slots_of = brick_slot.reshape(-1)
    slot_table = porosity.reshape(-1)
    brick_hit = (listed[:, None] == jnp.arange(brick_count, dtype=jnp.int32)[None, :]).astype(
        jnp.float32
    )
    slot_hit = (
        slots_of[:, None] == jnp.arange(slot_table.shape[0], dtype=jnp.int32)[None, :]
    ).astype(jnp.float32)

    def shift(value, axis, size, step):
        return lax.ppermute(value, axis, [(i, (i + step) % size) for i in range(size)])

    cot32 = cotangent.astype(jnp.float32)
    plane_count = (2 * q_count + 1) * layers_dev
    groups = -(-plane_count // (cols_dev // 4))
    smem = pl.BlockSpec(memory_space=pltpu.SMEM)
    packed, solid = pl.pallas_call(
        pack_kernel,
        out_shape=(
            jax.ShapeDtypeStruct((groups, rows_dev, cols_dev), jnp.float32),
            jax.ShapeDtypeStruct((layers_dev, rows_dev, cols_dev), jnp.float32),
        ),
        in_specs=vmem_specs(2) + [smem, smem, smem],
        out_specs=tuple(vmem_specs(2)),
        scratch_shapes=[pltpu.SMEM((brick_count,), jnp.float32)],
    )(f_start, cotangent, slot_table, listed, slots_of)
    from_left = shift(packed, "gx", nx, 1)
    from_right = shift(packed, "gx", nx, -1)

    def edge_rows(chosen):
        rows = jnp.concatenate([f_start[:, :, chosen], cot32[:, :, chosen], solid[None, :, chosen]], axis=0)
        corners = jnp.concatenate([from_left[:, chosen], from_right[:, chosen]], axis=0)
        return jnp.concatenate(
            [rows.reshape(-1, cols_dev), corners.reshape(-1, cols_dev)], axis=0
        )

    first_rows = edge_rows(slice(0, 2))
    last_rows = edge_rows(slice(rows_dev - 2, rows_dev))
    up_rows = shift(last_rows, "gy", ny, 1)
    dn_rows = shift(first_rows, "gy", ny, -1)
    big = pltpu.VMEM((q_count, layers_dev, ROWS, LANES), jnp.float32)
    start_grad, solid_bar = pl.pallas_call(
        compute_kernel,
        out_shape=(
            jax.ShapeDtypeStruct(f_start.shape, jnp.float32),
            jax.ShapeDtypeStruct(solid.shape, jnp.float32),
        ),
        in_specs=[pl.BlockSpec(memory_space=pl.ANY)] * 2 + vmem_specs(5),
        out_specs=tuple(vmem_specs(2)),
        scratch_shapes=[
            big,
            big,
            pltpu.VMEM((layers_dev, ROWS, LANES), jnp.float32),
            big,
            pltpu.VMEM((q_count, layers_dev, ROWS - 8, LANES), jnp.float32),
            pltpu.VMEM((layers_dev, ROWS - 8, LANES), jnp.float32),
            pltpu.VMEM(f_start.shape, jnp.float32),
            pltpu.VMEM(cotangent.shape, cotangent.dtype),
            pltpu.SemaphoreType.DMA((2,)),
        ],
        compiler_params=pltpu.CompilerParams(vmem_limit_bytes=48 * 1024 * 1024),
    )(f_start, cotangent, solid, up_rows, dn_rows, from_left, from_right)
    tile_sums = jnp.sum(solid_bar.reshape(brick_count, 128), axis=1)
    brick_sum = jnp.sum(brick_hit * tile_sums[None, :], axis=1)
    slot_grad = jnp.sum(slot_hit * brick_sum[:, None], axis=0)
    return (start_grad, slot_grad.reshape(porosity.shape))


def solution(mesh):
    return jax.shard_map(
        on_device,
        mesh=mesh,
        in_specs=(
            P(None, None, "gy", "gx"),
            P(None, None, "gy", "gx"),
            P("gx", "gy", None),
            P("gx", "gy", None),
            P("gx", "gy", None),
        ),
        out_specs=(P(None, None, "gy", "gx"), P("gx", "gy", None)),
        check_vma=False,
    )
```
